1024 devices in a mesh: tm: 64 (over y, x, z_hi), tensor: 16 (over z_lo, core).
Axes of the slice: x: 4, y: 8, z: 16 (z_hi: 2, z_lo: 8; z = z_hi * 8 + z_lo), core: 2. Of those that a mesh axis runs over, the one named last changes fastest.
Arguments:
- normed: bfloat16 [16384, 1536], P('tm'), may hold values from -24 to 24
- grad_out: bfloat16 [16384, 1536], P('tm'), may hold values from -4 to 4
- w_query: bfloat16 [1536, 1024], P(None, 'tensor'), may hold values from -0.15625 to 0.15625
- w_key: bfloat16 [1536, 1024], P(None, 'tensor'), may hold values from -0.15625 to 0.15625
- w_value: bfloat16 [1536, 1024], P(None, 'tensor'), may hold values from -0.15625 to 0.15625
- w_out: bfloat16 [1024, 1536], P('tensor'), may hold values from -0.1875 to 0.1875
- key_span: int32 [128, 16], replicated, may hold values from 0 to 127, as said below
Outputs:
- dnormed: float32 [16384, 1536], P('tm')
The draws below stay inside these ranges and needn't reach their ends.
Inputs may be any that keep to these rules, and one draw needn't show every extreme that they name: `key_span`: each reader span names distinct key spans. The key spans named by the 2 reader spans of one tm index lie on 32 distinct tm indices, one span on each, and the spans of each tm index are named by readers of exactly 32 tm indices.
All inputs are finite; a program needn't handle non-finite values.
Results may differ from the reference program's by a relative error of at most 0.014.
The reference program's roundings to bfloat16 on the way (of `dout`, `probs_b` and `dscores_b`) count: a program that leaves them out, or rounds other values in their place, can miss the bound.
Values may be sent and summed in bfloat16 or wider, within the bound.
No kernel may reach another device: no remote copies, remote signals or barrier semaphores. Data moves between devices by JAX's collectives and lax.ppermute only.
A program may use at most 32 MiB of HBM per device.

```python
import jax
import jax.numpy as jnp
from jax import lax

D = 1536
HEADS = 16
HD = 64
SPAN = 128
CPD = 2
KPR = 16
NCH = 128
FRAMES = 16384


def draw_key_span(key, part):
    device_count = NCH // CPD
    first_key, second_key, third_key = jax.random.split(key, 3)
    order = jax.random.permutation(first_key, device_count).astype(jnp.int32)
    ranking = jnp.zeros((device_count,), jnp.int32).at[order].set(jnp.arange(device_count, dtype=jnp.int32))
    offsets = jax.random.permutation(second_key, device_count).astype(jnp.int32)[:CPD * KPR]
    owners = order[(ranking[:, None] + offsets[None, :]) % device_count]
    within = jax.random.randint(third_key, (device_count, CPD * KPR), 0, CPD).astype(jnp.int32)
    within = within.at[:, 0].set(CPD - 1).at[:, 1].set(0)
    return (owners * CPD + within).reshape(device_count * CPD, KPR).astype(jnp.int32)


def draw_normed(key, part):
    first_key = jax.random.fold_in(key, 0)
    base = jnp.clip(jax.random.normal(first_key, (FRAMES, D), jnp.float32), -4.0, 4.0)
    return base.astype(jnp.bfloat16)


def block_levels(key, shape, shards, least, high):
    def one(axis_at, shards_of):
        steps = jax.random.uniform(jax.random.fold_in(jax.random.fold_in(key, 6), axis_at), (shards_of,), jnp.float32, least / len(shards), high / len(shards))
        return jnp.repeat(jnp.exp(steps), shape[axis_at] // shards_of).reshape((-1,) + (1,) * (len(shape) - axis_at - 1))

    level = one(*shards[0])
    for cut in shards[1:]:
        level = level * one(*cut)
    return level


def bell_draw(stream_key, extent, width, most, pieces=(), kind=jnp.bfloat16):
    entries = width * jax.random.normal(stream_key, extent, jnp.float32)
    if pieces:
        entries = entries * block_levels(stream_key, extent, pieces, -0.22, 0.18)
    return jnp.clip(entries, -most, most).astype(kind)


def setup_inputs(seed: int = 0) -> dict:
    seeds = jax.random.split(jax.random.key(seed), 8)
    return {
        "normed": draw_normed(jax.random.fold_in(seeds[7], 71), 0),
        "grad_out": bell_draw(seeds[1], (FRAMES, D), 1.0, 4.0, ((0, 64),)),
        "w_query": bell_draw(seeds[2], (D, HEADS * HD), D ** -0.5, 0.15625, ((1, 16),)),
        "w_key": bell_draw(seeds[3], (D, HEADS * HD), D ** -0.5, 0.15625, ((1, 16),)),
        "w_value": bell_draw(seeds[4], (D, HEADS * HD), D ** -0.5, 0.15625, ((1, 16),)),
        "w_out": bell_draw(seeds[5], (HEADS * HD, D), (HEADS * HD) ** -0.5, 0.1875, ((0, 16),)),
        "key_span": draw_key_span(jax.random.fold_in(seeds[7], 71), 0),
    }


def rounded(array_in):
    return lax.optimization_barrier(array_in.astype(jnp.bfloat16))

def attend_grad(query_rows, key_rows, value_rows, dout_rows):
    scaling = HD ** (-0.5)
    query_f = query_rows.astype(jnp.float32)
    key_f = key_rows.astype(jnp.float32)
    value_f = value_rows.astype(jnp.float32)
    dout_f = dout_rows.astype(jnp.float32)
    scores = jnp.einsum('qhd,khd->hqk', query_f, key_f) * scaling
    probs = jax.nn.softmax(scores, axis=-1)
    probs_b = rounded(probs).astype(jnp.float32)
    attn = jnp.einsum('hqk,khd->qhd', probs_b, value_f)
    delta = lax.optimization_barrier(jnp.sum(dout_f * attn, axis=-1)).T
    dprobs = jnp.einsum('qhd,khd->hqk', dout_f, value_f)
    dscores = probs * (dprobs - delta[:, :, None])
    dscores_b = rounded(dscores).astype(jnp.float32)
    grad_query = rounded(jnp.einsum('hqk,khd->qhd', dscores_b, key_f) * scaling)
    grad_key = rounded(jnp.einsum('hqk,qhd->khd', dscores_b, query_f) * scaling)
    grad_value = rounded(jnp.einsum('hqk,qhd->khd', probs_b, dout_f))
    return (grad_query, grad_key, grad_value)

def reference(normed, grad_out, w_query, w_key, w_value, w_out, key_span):
    queries = rounded(jnp.dot(normed, w_query, preferred_element_type=jnp.float32))
    keys_all = rounded(jnp.dot(normed, w_key, preferred_element_type=jnp.float32))
    values_all = rounded(jnp.dot(normed, w_value, preferred_element_type=jnp.float32))
    dout = rounded(jnp.dot(grad_out, w_out.T, preferred_element_type=jnp.float32))
    query_spans = queries.reshape(NCH, SPAN, HEADS, HD)
    key_spans = keys_all.reshape(NCH, SPAN, HEADS, HD)
    value_spans = values_all.reshape(NCH, SPAN, HEADS, HD)
    dout_spans = dout.reshape(NCH, SPAN, HEADS, HD)
    zeros_acc = jnp.zeros((NCH, SPAN, HEADS, HD), jnp.float32)

    def step_reader(carry, reader):
        key_acc, value_acc = carry
        chosen = key_span[reader]
        key_rows = key_spans[chosen].reshape(KPR * SPAN, HEADS, HD)
        value_rows = value_spans[chosen].reshape(KPR * SPAN, HEADS, HD)
        grad_query, grad_key, grad_value = attend_grad(query_spans[reader], key_rows, value_rows, dout_spans[reader])
        key_acc = key_acc.at[chosen].add(grad_key.reshape(KPR, SPAN, HEADS, HD).astype(jnp.float32))
        value_acc = value_acc.at[chosen].add(grad_value.reshape(KPR, SPAN, HEADS, HD).astype(jnp.float32))
        return ((key_acc, value_acc), grad_query)
    (key_acc, value_acc), grad_queries = lax.scan(step_reader, (zeros_acc, zeros_acc), jnp.arange(NCH, dtype=jnp.int32))
    grad_keys = key_acc.astype(jnp.bfloat16).reshape(FRAMES, HEADS * HD)
    grad_values = value_acc.astype(jnp.bfloat16).reshape(FRAMES, HEADS * HD)
    grad_queries = grad_queries.reshape(FRAMES, HEADS * HD)
    result = jnp.dot(grad_queries, w_query.T, preferred_element_type=jnp.float32)
    result = result + jnp.dot(grad_keys, w_key.T, preferred_element_type=jnp.float32)
    result = result + jnp.dot(grad_values, w_value.T, preferred_element_type=jnp.float32)
    return result
```

```python
import jax
import jax.numpy as jnp
from jax import lax
from jax.sharding import PartitionSpec as P

HD = 64
SPAN = 128


def attend_grad(query_t, key_t, value_t, dout_t):
    scaling = HD ** (-0.5)
    scores = (
        jnp.einsum("chdq,cjhdk->chqjk", query_t, key_t, preferred_element_type=jnp.float32)
        * scaling
    )
    probs = jax.nn.softmax(scores, axis=(-2, -1))
    probs_b = probs.astype(jnp.bfloat16)
    attn = jnp.einsum("chqjk,cjhdk->chdq", probs_b, value_t, preferred_element_type=jnp.float32)
    delta = jnp.sum(dout_t.astype(jnp.float32) * attn, axis=2)
    dprobs = jnp.einsum("chdq,cjhdk->chqjk", dout_t, value_t, preferred_element_type=jnp.float32)
    dscores_b = (probs * (dprobs - delta[:, :, :, None, None])).astype(jnp.bfloat16)
    grad_query = (
        jnp.einsum("chqjk,cjhdk->chdq", dscores_b, key_t, preferred_element_type=jnp.float32)
        * scaling
    ).astype(jnp.bfloat16)
    grad_key = (
        jnp.einsum("chqjk,chdq->cjhdk", dscores_b, query_t, preferred_element_type=jnp.float32)
        * scaling
    ).astype(jnp.bfloat16)
    grad_value = jnp.einsum(
        "chqjk,chdq->cjhdk", probs_b, dout_t, preferred_element_type=jnp.float32
    ).astype(jnp.bfloat16)
    return (grad_query, grad_key, grad_value)


def project_back(grads_t, weight):
    return lax.dot_general(
        grads_t, weight, (((0,), (1,)), ((), ())), preferred_element_type=jnp.float32
    )


def project_cols(weight, inputs):
    return lax.dot_general(
        weight, inputs, (((0,), (1,)), ((), ())), preferred_element_type=jnp.float32
    )


def local(normed, grad_out, w_query, w_key, w_value, w_out, key_span):
    device_count = lax.axis_size("tm")
    my_index = lax.axis_index("tm")
    row_count = normed.shape[0]
    col_count = w_query.shape[1]
    head_count = col_count // HD
    owned = row_count // SPAN
    per_reader = key_span.shape[1]
    queries_t = project_cols(w_query, normed).astype(jnp.bfloat16)
    keys_t = project_cols(w_key, normed).astype(jnp.bfloat16)
    values_t = project_cols(w_value, normed).astype(jnp.bfloat16)
    dout_t = lax.dot_general(
        w_out, grad_out, (((1,), (1,)), ((), ())), preferred_element_type=jnp.float32
    ).astype(jnp.bfloat16)
    paired_t = jnp.concatenate([keys_t, values_t], axis=0)
    paired_spans = jnp.transpose(paired_t.reshape(2 * col_count, owned, SPAN), (1, 0, 2))
    all_pairs = key_span.reshape(device_count, owned * per_reader)
    hits = all_pairs // owned == my_index
    slot_match = (all_pairs % owned)[:, :, None] == jnp.arange(owned, dtype=jnp.int32)[
        None, None, :
    ]
    picked = jnp.sum((hits[:, :, None] & slot_match).astype(jnp.int32), axis=1).astype(jnp.bfloat16)
    own_ids = lax.dynamic_slice_in_dim(key_span, my_index * owned, owned, 0)
    owner_ids = (own_ids // owned).reshape(-1)
    asked = jnp.sum(jnp.where(hits, all_pairs % owned, 0), axis=1)
    outgoing = paired_spans[asked]
    incoming = lax.all_to_all(outgoing, "tm", split_axis=0, concat_axis=0, tiled=True)
    fetched = incoming[owner_ids]
    fetched = fetched.reshape(owned, per_reader, 2, head_count, HD, SPAN)
    query_rows = jnp.transpose(queries_t.reshape(head_count, HD, owned, SPAN), (2, 0, 1, 3))
    dout_rows = jnp.transpose(dout_t.reshape(head_count, HD, owned, SPAN), (2, 0, 1, 3))
    grad_query, grad_key, grad_value = attend_grad(
        query_rows, fetched[:, :, 0], fetched[:, :, 1], dout_rows
    )
    grad_query_t = jnp.transpose(grad_query, (1, 2, 0, 3)).reshape(col_count, row_count)
    query_term = project_back(grad_query_t, w_query)
    pair_grads = jnp.concatenate(
        [
            grad_key.reshape(owned * per_reader, col_count, SPAN),
            grad_value.reshape(owned * per_reader, col_count, SPAN),
        ],
        axis=1,
    )
    returned = (
        jnp.zeros((device_count, 2 * col_count, SPAN), jnp.bfloat16).at[owner_ids].set(pair_grads)
    )
    received = lax.all_to_all(returned, "tm", split_axis=0, concat_axis=0, tiled=True)
    summed = jnp.einsum("nc,nrh->crh", picked, received, preferred_element_type=jnp.float32).astype(
        jnp.bfloat16
    )
    summed_t = jnp.transpose(summed, (1, 0, 2)).reshape(2 * col_count, row_count)
    kv_term = project_back(summed_t[:col_count], w_key) + project_back(
        summed_t[col_count:], w_value
    )
    result = lax.psum(query_term + kv_term, "tensor")
    return result


def solution(mesh):
    return jax.shard_map(
        local,
        mesh=mesh,
        in_specs=(
            P("tm", None),
            P("tm", None),
            P(None, "tensor"),
            P(None, "tensor"),
            P(None, "tensor"),
            P("tensor", None),
            P(),
        ),
        out_specs=P("tm", None),
        check_vma=False,
    )
```

```python
import jax
import jax.numpy as jnp
from jax import lax
from jax.sharding import PartitionSpec as P

HD = 64
SPAN = 128


def attend_grad(query_t, key_t, value_t, dout_t):
    scaling = HD ** (-0.5)
    scores = (
        jnp.einsum("chdq,cjhdk->chqjk", query_t, key_t, preferred_element_type=jnp.float32)
        * scaling
    )
    probs = jax.nn.softmax(scores, axis=(-2, -1))
    probs_b = probs.astype(jnp.bfloat16)
    attn = jnp.einsum("chqjk,cjhdk->chdq", probs_b, value_t, preferred_element_type=jnp.float32)
    delta = jnp.sum(dout_t.astype(jnp.float32) * attn, axis=2)
    dprobs = jnp.einsum("chdq,cjhdk->chqjk", dout_t, value_t, preferred_element_type=jnp.float32)
    dscores_b = (probs * (dprobs - delta[:, :, :, None, None])).astype(jnp.bfloat16)
    grad_query = (
        jnp.einsum("chqjk,cjhdk->chdq", dscores_b, key_t, preferred_element_type=jnp.float32)
        * scaling
    ).astype(jnp.bfloat16)
    grad_key = (
        jnp.einsum("chqjk,chdq->cjhdk", dscores_b, query_t, preferred_element_type=jnp.float32)
        * scaling
    ).astype(jnp.bfloat16)
    grad_value = jnp.einsum(
        "chqjk,chdq->cjhdk", probs_b, dout_t, preferred_element_type=jnp.float32
    ).astype(jnp.bfloat16)
    return (grad_query, grad_key, grad_value)


def project_back(grads_t, weight):
    return lax.dot_general(
        grads_t, weight, (((0,), (1,)), ((), ())), preferred_element_type=jnp.float32
    )


def project_cols(weight, inputs):
    return lax.dot_general(
        weight, inputs, (((0,), (1,)), ((), ())), preferred_element_type=jnp.float32
    )


def head_sum(partial):
    index = lax.axis_index("tensor")
    count = lax.axis_size("tensor")
    cur = partial
    step = 1
    while step < count:
        upper = (index & step) != 0
        half = cur.shape[0] // 2
        low, high = cur[:half], cur[half:]
        keep = jnp.where(upper, high, low)
        send = jnp.where(upper, low, high)
        got = lax.ppermute(send, "tensor", [(i, i ^ step) for i in range(count)])
        cur = keep + got
        step *= 2
    while step > 1:
        step //= 2
        upper = (index & step) != 0
        got = lax.ppermute(cur, "tensor", [(i, i ^ step) for i in range(count)])
        cur = jnp.where(upper, jnp.concatenate([got, cur]), jnp.concatenate([cur, got]))
    return cur


def local(normed, grad_out, w_query, w_key, w_value, w_out, key_span):
    device_count = lax.axis_size("tm")
    my_index = lax.axis_index("tm")
    row_count = normed.shape[0]
    col_count = w_query.shape[1]
    head_count = col_count // HD
    owned = row_count // SPAN
    per_reader = key_span.shape[1]
    queries_t = project_cols(w_query, normed).astype(jnp.bfloat16)
    keys_t = project_cols(w_key, normed).astype(jnp.bfloat16)
    values_t = project_cols(w_value, normed).astype(jnp.bfloat16)
    dout_t = lax.dot_general(
        w_out, grad_out, (((1,), (1,)), ((), ())), preferred_element_type=jnp.float32
    ).astype(jnp.bfloat16)
    paired_t = jnp.concatenate([keys_t, values_t], axis=0)
    paired_spans = jnp.transpose(paired_t.reshape(2 * col_count, owned, SPAN), (1, 0, 2))
    all_pairs = key_span.reshape(device_count, owned * per_reader)
    hits = all_pairs // owned == my_index
    slot_match = (all_pairs % owned)[:, :, None] == jnp.arange(owned, dtype=jnp.int32)[
        None, None, :
    ]
    picked = jnp.sum((hits[:, :, None] & slot_match).astype(jnp.int32), axis=1).astype(jnp.bfloat16)
    own_ids = lax.dynamic_slice_in_dim(key_span, my_index * owned, owned, 0)
    owner_ids = (own_ids // owned).reshape(-1)
    asked = jnp.sum(jnp.where(hits, all_pairs % owned, 0), axis=1)
    outgoing = paired_spans[asked]
    incoming = lax.all_to_all(outgoing, "tm", split_axis=0, concat_axis=0, tiled=True)
    fetched = incoming[owner_ids]
    fetched = fetched.reshape(owned, per_reader, 2, head_count, HD, SPAN)
    query_rows = jnp.transpose(queries_t.reshape(head_count, HD, owned, SPAN), (2, 0, 1, 3))
    dout_rows = jnp.transpose(dout_t.reshape(head_count, HD, owned, SPAN), (2, 0, 1, 3))
    grad_query, grad_key, grad_value = attend_grad(
        query_rows, fetched[:, :, 0], fetched[:, :, 1], dout_rows
    )
    grad_query_t = jnp.transpose(grad_query, (1, 2, 0, 3)).reshape(col_count, row_count)
    query_term = project_back(grad_query_t, w_query)
    pair_grads = jnp.concatenate(
        [
            grad_key.reshape(owned * per_reader, col_count, SPAN),
            grad_value.reshape(owned * per_reader, col_count, SPAN),
        ],
        axis=1,
    )
    returned = (
        jnp.zeros((device_count, 2 * col_count, SPAN), jnp.bfloat16).at[owner_ids].set(pair_grads)
    )
    received = lax.all_to_all(returned, "tm", split_axis=0, concat_axis=0, tiled=True)
    summed = jnp.einsum("nc,nrh->crh", picked, received, preferred_element_type=jnp.float32).astype(
        jnp.bfloat16
    )
    summed_t = jnp.transpose(summed, (1, 0, 2)).reshape(2 * col_count, row_count)
    kv_term = project_back(summed_t[:col_count], w_key) + project_back(
        summed_t[col_count:], w_value
    )
    result = head_sum(query_term + kv_term)
    return result


def solution(mesh):
    return jax.shard_map(
        local,
        mesh=mesh,
        in_specs=(
            P("tm", None),
            P("tm", None),
            P(None, "tensor"),
            P(None, "tensor"),
            P(None, "tensor"),
            P("tensor", None),
            P(),
        ),
        out_specs=P("tm", None),
        check_vma=False,
    )
```

```python
import jax
import jax.numpy as jnp
from jax import lax
from jax.sharding import Mesh, PartitionSpec as P

HD = 64
SPAN = 128


def attend_grad(query_t, key_t, value_t, dout_t):
    scaling = HD ** (-0.5)
    scores = (
        jnp.einsum("chdq,cjhdk->chqjk", query_t, key_t, preferred_element_type=jnp.float32)
        * scaling
    )
    probs = jax.nn.softmax(scores, axis=(-2, -1))
    probs_b = probs.astype(jnp.bfloat16)
    attn = jnp.einsum("chqjk,cjhdk->chdq", probs_b, value_t, preferred_element_type=jnp.float32)
    delta = jnp.sum(dout_t.astype(jnp.float32) * attn, axis=2)
    dprobs = jnp.einsum("chdq,cjhdk->chqjk", dout_t, value_t, preferred_element_type=jnp.float32)
    dscores_b = (probs * (dprobs - delta[:, :, :, None, None])).astype(jnp.bfloat16)
    grad_query = (
        jnp.einsum("chqjk,cjhdk->chdq", dscores_b, key_t, preferred_element_type=jnp.float32)
        * scaling
    ).astype(jnp.bfloat16)
    grad_key = (
        jnp.einsum("chqjk,chdq->cjhdk", dscores_b, query_t, preferred_element_type=jnp.float32)
        * scaling
    ).astype(jnp.bfloat16)
    grad_value = jnp.einsum(
        "chqjk,chdq->cjhdk", probs_b, dout_t, preferred_element_type=jnp.float32
    ).astype(jnp.bfloat16)
    return (grad_query, grad_key, grad_value)


def project_back(grads_t, weight):
    return lax.dot_general(
        grads_t, weight, (((0,), (1,)), ((), ())), preferred_element_type=jnp.float32
    )


def project_cols(weight, inputs):
    return lax.dot_general(
        weight, inputs, (((0,), (1,)), ((), ())), preferred_element_type=jnp.float32
    )


def head_sum(partial):
    index = lax.axis_index("tensor")
    count = lax.axis_size("tensor")
    cur = partial
    step = 1
    while step < count:
        upper = (index & step) != 0
        half = cur.shape[0] // 2
        low, high = cur[:half], cur[half:]
        keep = jnp.where(upper, high, low)
        send = jnp.where(upper, low, high)
        got = lax.ppermute(send, "tensor", [(i, i ^ step) for i in range(count)])
        cur = keep + got
        step *= 2
    while step > 1:
        step //= 2
        upper = (index & step) != 0
        got = lax.ppermute(cur, "tensor", [(i, i ^ step) for i in range(count)])
        cur = jnp.where(upper, jnp.concatenate([got, cur]), jnp.concatenate([cur, got]))
    return cur


def local(normed, grad_out, w_query, w_key, w_value, w_out, key_span):
    column_count = lax.axis_size("tq")
    side_count = lax.axis_size("zh")
    my_column = lax.axis_index("tq")
    my_side = lax.axis_index("zh")
    device_count = column_count * side_count
    my_index = my_column * side_count + my_side
    swap = [(0, 1), (1, 0)]
    row_count = normed.shape[0]
    col_count = w_query.shape[1]
    head_count = col_count // HD
    owned = row_count // SPAN
    per_reader = key_span.shape[1]
    queries_t = project_cols(w_query, normed).astype(jnp.bfloat16)
    keys_t = project_cols(w_key, normed).astype(jnp.bfloat16)
    values_t = project_cols(w_value, normed).astype(jnp.bfloat16)
    dout_t = lax.dot_general(
        w_out, grad_out, (((1,), (1,)), ((), ())), preferred_element_type=jnp.float32
    ).astype(jnp.bfloat16)
    paired_t = jnp.concatenate([keys_t, values_t], axis=0)
    paired_spans = jnp.transpose(paired_t.reshape(2 * col_count, owned, SPAN), (1, 0, 2))
    mirror_spans = lax.ppermute(paired_spans, "zh", swap)
    have = jnp.where(
        my_side == 0,
        jnp.concatenate([paired_spans, mirror_spans]),
        jnp.concatenate([mirror_spans, paired_spans]),
    )
    all_pairs = key_span.reshape(column_count, side_count, owned * per_reader)
    requests = lax.dynamic_index_in_dim(all_pairs, my_side, axis=1, keepdims=False)
    sides = my_column * side_count + jnp.arange(side_count, dtype=jnp.int32)
    hit = (requests // owned)[:, :, None] == sides[None, None, :]
    slot = jnp.sum(jnp.where(hit, (requests % owned)[:, :, None], 0), axis=1)
    exists = jnp.any(hit, axis=1)
    which = jnp.arange(side_count, dtype=jnp.int32)[None, :] * owned + slot
    outgoing = have[which.reshape(-1)]
    incoming = lax.all_to_all(outgoing, "tq", split_axis=0, concat_axis=0, tiled=True)
    own_ids = lax.dynamic_slice_in_dim(key_span, my_index * owned, owned, 0)
    owner_ids = (own_ids // owned).reshape(-1)
    fetched = incoming[owner_ids]
    fetched = fetched.reshape(owned, per_reader, 2, head_count, HD, SPAN)
    query_rows = jnp.transpose(queries_t.reshape(head_count, HD, owned, SPAN), (2, 0, 1, 3))
    dout_rows = jnp.transpose(dout_t.reshape(head_count, HD, owned, SPAN), (2, 0, 1, 3))
    grad_query, grad_key, grad_value = attend_grad(
        query_rows, fetched[:, :, 0], fetched[:, :, 1], dout_rows
    )
    grad_query_t = jnp.transpose(grad_query, (1, 2, 0, 3)).reshape(col_count, row_count)
    query_term = project_back(grad_query_t, w_query)
    pair_grads = jnp.concatenate(
        [
            grad_key.reshape(owned * per_reader, col_count, SPAN),
            grad_value.reshape(owned * per_reader, col_count, SPAN),
        ],
        axis=1,
    )
    returned = (
        jnp.zeros((device_count, 2 * col_count, SPAN), jnp.bfloat16).at[owner_ids].set(pair_grads)
    )
    received = lax.all_to_all(returned, "tq", split_axis=0, concat_axis=0, tiled=True)
    received = received.reshape(column_count, side_count, 2 * col_count, SPAN)
    picked = (
        exists[:, :, None] & (slot[:, :, None] == jnp.arange(owned, dtype=jnp.int32)[None, None, :])
    ).astype(jnp.bfloat16)
    partial = jnp.einsum("csk,csrh->skrh", picked, received, preferred_element_type=jnp.float32)
    mine = lax.dynamic_index_in_dim(partial, my_side, axis=0, keepdims=False)
    other = lax.dynamic_index_in_dim(partial, 1 - my_side, axis=0, keepdims=False)
    summed = (mine + lax.ppermute(other, "zh", swap)).astype(jnp.bfloat16)
    summed_t = jnp.transpose(summed, (1, 0, 2)).reshape(2 * col_count, row_count)
    kv_term = project_back(summed_t[:col_count], w_key) + project_back(
        summed_t[col_count:], w_value
    )
    result = head_sum(query_term + kv_term)
    return result


def solution(mesh):
    tm_size = mesh.shape["tm"]
    tensor_size = mesh.shape["tensor"]
    split = Mesh(mesh.devices.reshape(tm_size // 2, 2, tensor_size), ("tq", "zh", "tensor"))
    rows = P(("tq", "zh"), None)
    return jax.shard_map(
        local,
        mesh=split,
        in_specs=(
            rows,
            rows,
            P(None, "tensor"),
            P(None, "tensor"),
            P(None, "tensor"),
            P("tensor", None),
            P(),
        ),
        out_specs=rows,
        check_vma=False,
    )
```

```python
import jax
import jax.numpy as jnp
from jax import lax
from jax.sharding import Mesh, PartitionSpec as P

HD = 64
SPAN = 128


def attend_grad(query_t, key_t, value_t, dout_t):
    scaling = HD ** (-0.5)
    scores = (
        jnp.einsum("chdq,cjhdk->chqjk", query_t, key_t, preferred_element_type=jnp.float32)
        * scaling
    )
    probs = jax.nn.softmax(scores, axis=(-2, -1))
    probs_b = probs.astype(jnp.bfloat16)
    attn = jnp.einsum("chqjk,cjhdk->chdq", probs_b, value_t, preferred_element_type=jnp.float32)
    delta = jnp.sum(dout_t.astype(jnp.float32) * attn, axis=2)
    dprobs = jnp.einsum("chdq,cjhdk->chqjk", dout_t, value_t, preferred_element_type=jnp.float32)
    dscores_b = (probs * (dprobs - delta[:, :, :, None, None])).astype(jnp.bfloat16)
    grad_query = (
        jnp.einsum("chqjk,cjhdk->chdq", dscores_b, key_t, preferred_element_type=jnp.float32)
        * scaling
    ).astype(jnp.bfloat16)
    grad_key = (
        jnp.einsum("chqjk,chdq->cjhdk", dscores_b, query_t, preferred_element_type=jnp.float32)
        * scaling
    ).astype(jnp.bfloat16)
    grad_value = jnp.einsum(
        "chqjk,chdq->cjhdk", probs_b, dout_t, preferred_element_type=jnp.float32
    ).astype(jnp.bfloat16)
    return (grad_query, grad_key, grad_value)


def project_back(grads_t, weight):
    return lax.dot_general(
        grads_t, weight, (((0,), (1,)), ((), ())), preferred_element_type=jnp.float32
    )


def project_cols(weight, inputs):
    return lax.dot_general(
        weight, inputs, (((0,), (1,)), ((), ())), preferred_element_type=jnp.float32
    )


def head_sum(partial):
    index = lax.axis_index("tensor")
    count = lax.axis_size("tensor")
    cur = partial
    step = 1
    while step < count:
        upper = (index & step) != 0
        half = cur.shape[0] // 2
        low, high = cur[:half], cur[half:]
        keep = jnp.where(upper, high, low)
        send = jnp.where(upper, low, high)
        got = lax.ppermute(send.astype(jnp.bfloat16), "tensor", [(i, i ^ step) for i in range(count)])
        cur = keep + got.astype(jnp.float32)
        step *= 2
    cur = cur.astype(jnp.bfloat16)
    while step > 1:
        step //= 2
        upper = (index & step) != 0
        got = lax.ppermute(cur, "tensor", [(i, i ^ step) for i in range(count)])
        cur = jnp.where(upper, jnp.concatenate([got, cur]), jnp.concatenate([cur, got]))
    return cur.astype(jnp.float32)


def local(normed, grad_out, w_query, w_key, w_value, w_out, key_span):
    column_count = lax.axis_size("tq")
    side_count = lax.axis_size("zh")
    my_column = lax.axis_index("tq")
    my_side = lax.axis_index("zh")
    device_count = column_count * side_count
    my_index = my_column * side_count + my_side
    swap = [(0, 1), (1, 0)]
    row_count = normed.shape[0]
    col_count = w_query.shape[1]
    head_count = col_count // HD
    owned = row_count // SPAN
    per_reader = key_span.shape[1]
    queries_t = project_cols(w_query, normed).astype(jnp.bfloat16)
    keys_t = project_cols(w_key, normed).astype(jnp.bfloat16)
    values_t = project_cols(w_value, normed).astype(jnp.bfloat16)
    dout_t = lax.dot_general(
        w_out, grad_out, (((1,), (1,)), ((), ())), preferred_element_type=jnp.float32
    ).astype(jnp.bfloat16)
    paired_t = jnp.concatenate([keys_t, values_t], axis=0)
    paired_spans = jnp.transpose(paired_t.reshape(2 * col_count, owned, SPAN), (1, 0, 2))
    mirror_spans = lax.ppermute(paired_spans, "zh", swap)
    have = jnp.where(
        my_side == 0,
        jnp.concatenate([paired_spans, mirror_spans]),
        jnp.concatenate([mirror_spans, paired_spans]),
    )
    all_pairs = key_span.reshape(column_count, side_count, owned * per_reader)
    requests = lax.dynamic_index_in_dim(all_pairs, my_side, axis=1, keepdims=False)
    sides = my_column * side_count + jnp.arange(side_count, dtype=jnp.int32)
    hit = (requests // owned)[:, :, None] == sides[None, None, :]
    slot = jnp.sum(jnp.where(hit, (requests % owned)[:, :, None], 0), axis=1)
    exists = jnp.any(hit, axis=1)
    which = jnp.arange(side_count, dtype=jnp.int32)[None, :] * owned + slot
    outgoing = have[which.reshape(-1)]
    incoming = lax.all_to_all(outgoing, "tq", split_axis=0, concat_axis=0, tiled=True)
    own_ids = lax.dynamic_slice_in_dim(key_span, my_index * owned, owned, 0)
    owner_ids = (own_ids // owned).reshape(-1)
    fetched = incoming[owner_ids]
    fetched = fetched.reshape(owned, per_reader, 2, head_count, HD, SPAN)
    query_rows = jnp.transpose(queries_t.reshape(head_count, HD, owned, SPAN), (2, 0, 1, 3))
    dout_rows = jnp.transpose(dout_t.reshape(head_count, HD, owned, SPAN), (2, 0, 1, 3))
    grad_query, grad_key, grad_value = attend_grad(
        query_rows, fetched[:, :, 0], fetched[:, :, 1], dout_rows
    )
    grad_query_t = jnp.transpose(grad_query, (1, 2, 0, 3)).reshape(col_count, row_count)
    query_term = project_back(grad_query_t, w_query)
    pair_grads = jnp.concatenate(
        [
            grad_key.reshape(owned * per_reader, col_count, SPAN),
            grad_value.reshape(owned * per_reader, col_count, SPAN),
        ],
        axis=1,
    )
    returned = (
        jnp.zeros((device_count, 2 * col_count, SPAN), jnp.bfloat16).at[owner_ids].set(pair_grads)
    )
    received = lax.all_to_all(returned, "tq", split_axis=0, concat_axis=0, tiled=True)
    received = received.reshape(column_count, side_count, 2 * col_count, SPAN)
    picked = (
        exists[:, :, None] & (slot[:, :, None] == jnp.arange(owned, dtype=jnp.int32)[None, None, :])
    ).astype(jnp.bfloat16)
    partial = jnp.einsum("csk,csrh->skrh", picked, received, preferred_element_type=jnp.float32)
    mine = lax.dynamic_index_in_dim(partial, my_side, axis=0, keepdims=False)
    other = lax.dynamic_index_in_dim(partial, 1 - my_side, axis=0, keepdims=False)
    summed = (mine + lax.ppermute(other, "zh", swap)).astype(jnp.bfloat16)
    summed_t = jnp.transpose(summed, (1, 0, 2)).reshape(2 * col_count, row_count)
    kv_term = project_back(summed_t[:col_count], w_key) + project_back(
        summed_t[col_count:], w_value
    )
    result = head_sum(query_term + kv_term)
    return result


def solution(mesh):
    tm_size = mesh.shape["tm"]
    tensor_size = mesh.shape["tensor"]
    split = Mesh(mesh.devices.reshape(tm_size // 2, 2, tensor_size), ("tq", "zh", "tensor"))
    rows = P(("tq", "zh"), None)
    return jax.shard_map(
        local,
        mesh=split,
        in_specs=(
            rows,
            rows,
            P(None, "tensor"),
            P(None, "tensor"),
            P(None, "tensor"),
            P("tensor", None),
            P(),
        ),
        out_specs=rows,
        check_vma=False,
    )
```

```python
import jax
import jax.numpy as jnp
from jax import lax
from jax.sharding import Mesh, PartitionSpec as P

HD = 64
SPAN = 128


def attend_grad(query_t, key_t, value_t, dout_t):
    scaling = HD ** (-0.5)
    scores = (
        jnp.einsum("chdq,cjhdk->chqjk", query_t, key_t, preferred_element_type=jnp.float32)
        * scaling
    )
    probs = jax.nn.softmax(scores, axis=(-2, -1))
    probs_b = probs.astype(jnp.bfloat16)
    attn = jnp.einsum("chqjk,cjhdk->chdq", probs_b, value_t, preferred_element_type=jnp.float32)
    delta = jnp.sum(dout_t.astype(jnp.float32) * attn, axis=2)
    dprobs = jnp.einsum("chdq,cjhdk->chqjk", dout_t, value_t, preferred_element_type=jnp.float32)
    dscores_b = (probs * (dprobs - delta[:, :, :, None, None])).astype(jnp.bfloat16)
    grad_query = (
        jnp.einsum("chqjk,cjhdk->chdq", dscores_b, key_t, preferred_element_type=jnp.float32)
        * scaling
    ).astype(jnp.bfloat16)
    grad_key = (
        jnp.einsum("chqjk,chdq->cjhdk", dscores_b, query_t, preferred_element_type=jnp.float32)
        * scaling
    ).astype(jnp.bfloat16)
    grad_value = jnp.einsum(
        "chqjk,chdq->cjhdk", probs_b, dout_t, preferred_element_type=jnp.float32
    ).astype(jnp.bfloat16)
    return (grad_query, grad_key, grad_value)


def project_back(grads_t, weight):
    return lax.dot_general(
        grads_t, weight, (((0,), (1,)), ((), ())), preferred_element_type=jnp.float32
    )


def project_cols(weight, inputs):
    return lax.dot_general(
        weight, inputs, (((0,), (1,)), ((), ())), preferred_element_type=jnp.float32
    )


def head_sum(partial):
    index = lax.axis_index("tensor")
    count = lax.axis_size("tensor")
    cur = partial
    step = 1
    while step < count:
        upper = (index & step) != 0
        half = cur.shape[0] // 2
        low, high = cur[:half], cur[half:]
        keep = jnp.where(upper, high, low)
        send = jnp.where(upper, low, high)
        got = lax.ppermute(send.astype(jnp.bfloat16), "tensor", [(i, i ^ step) for i in range(count)])
        cur = keep + got.astype(jnp.float32)
        step *= 2
    cur = cur.astype(jnp.bfloat16)
    while step > 1:
        step //= 2
        upper = (index & step) != 0
        got = lax.ppermute(cur, "tensor", [(i, i ^ step) for i in range(count)])
        cur = jnp.where(upper, jnp.concatenate([got, cur]), jnp.concatenate([cur, got]))
    return cur.astype(jnp.float32)


def local(normed, grad_out, w_query, w_key, w_value, w_out, key_span):
    column_count = lax.axis_size("tq")
    side_count = lax.axis_size("zh")
    my_column = lax.axis_index("tq")
    my_side = lax.axis_index("zh")
    device_count = column_count * side_count
    my_index = my_column * side_count + my_side
    swap = [(0, 1), (1, 0)]
    row_count = normed.shape[0]
    col_count = w_query.shape[1]
    head_count = col_count // HD
    owned = row_count // SPAN
    per_reader = key_span.shape[1]
    queries_t = project_cols(w_query, normed).astype(jnp.bfloat16)
    keys_t = project_cols(w_key, normed).astype(jnp.bfloat16)
    values_t = project_cols(w_value, normed).astype(jnp.bfloat16)
    dout_t = lax.dot_general(
        w_out, grad_out, (((1,), (1,)), ((), ())), preferred_element_type=jnp.float32
    ).astype(jnp.bfloat16)
    paired_t = jnp.concatenate([keys_t, values_t], axis=0)
    paired_spans = jnp.transpose(paired_t.reshape(2 * col_count, owned, SPAN), (1, 0, 2))
    mirror_spans = lax.ppermute(paired_spans, "zh", swap)
    all_pairs = key_span.reshape(column_count, side_count, owned * per_reader)
    requests = lax.dynamic_index_in_dim(all_pairs, my_side, axis=1, keepdims=False)
    sides = my_column * side_count + jnp.arange(side_count, dtype=jnp.int32)
    hit = (requests // owned)[:, :, None] == sides[None, None, :]
    slot = jnp.sum(jnp.where(hit, (requests % owned)[:, :, None], 0), axis=1)
    exists = jnp.any(hit, axis=1)
    own_slot = lax.dynamic_index_in_dim(slot, my_side, axis=1, keepdims=False)
    mirror_slot = lax.dynamic_index_in_dim(slot, 1 - my_side, axis=1, keepdims=False)
    near = lax.all_to_all(paired_spans[own_slot], "tq", split_axis=0, concat_axis=0, tiled=True)
    far = lax.all_to_all(mirror_spans[mirror_slot], "tq", split_axis=0, concat_axis=0, tiled=True)
    incoming = jnp.where(
        my_side == 0, jnp.stack([near, far], axis=1), jnp.stack([far, near], axis=1)
    ).reshape(device_count, 2 * col_count, SPAN)
    own_ids = lax.dynamic_slice_in_dim(key_span, my_index * owned, owned, 0)
    owner_ids = (own_ids // owned).reshape(-1)
    fetched = incoming[owner_ids]
    fetched = fetched.reshape(owned, per_reader, 2, head_count, HD, SPAN)
    query_rows = jnp.transpose(queries_t.reshape(head_count, HD, owned, SPAN), (2, 0, 1, 3))
    dout_rows = jnp.transpose(dout_t.reshape(head_count, HD, owned, SPAN), (2, 0, 1, 3))
    grad_query, grad_key, grad_value = attend_grad(
        query_rows, fetched[:, :, 0], fetched[:, :, 1], dout_rows
    )
    grad_query_t = jnp.transpose(grad_query, (1, 2, 0, 3)).reshape(col_count, row_count)
    query_term = project_back(grad_query_t, w_query)
    pair_grads = jnp.concatenate(
        [
            grad_key.reshape(owned * per_reader, col_count, SPAN),
            grad_value.reshape(owned * per_reader, col_count, SPAN),
        ],
        axis=1,
    )
    returned = (
        jnp.zeros((device_count, 2 * col_count, SPAN), jnp.bfloat16).at[owner_ids].set(pair_grads)
    )
    returned = returned.reshape(column_count, side_count, 2 * col_count, SPAN)
    picked = (
        exists[:, :, None] & (slot[:, :, None] == jnp.arange(owned, dtype=jnp.int32)[None, None, :])
    ).astype(jnp.bfloat16)
    far_back = lax.all_to_all(
        lax.dynamic_index_in_dim(returned, 1 - my_side, axis=1, keepdims=False),
        "tq", split_axis=0, concat_axis=0, tiled=True,
    )
    other = jnp.einsum(
        "ck,crh->krh",
        lax.dynamic_index_in_dim(picked, 1 - my_side, axis=1, keepdims=False),
        far_back,
        preferred_element_type=jnp.float32,
    )
    other_back = lax.ppermute(other, "zh", swap)
    near_back = lax.all_to_all(
        lax.dynamic_index_in_dim(returned, my_side, axis=1, keepdims=False),
        "tq", split_axis=0, concat_axis=0, tiled=True,
    )
    mine = jnp.einsum(
        "ck,crh->krh",
        lax.dynamic_index_in_dim(picked, my_side, axis=1, keepdims=False),
        near_back,
        preferred_element_type=jnp.float32,
    )
    summed = (mine + other_back).astype(jnp.bfloat16)
    summed_t = jnp.transpose(summed, (1, 0, 2)).reshape(2 * col_count, row_count)
    kv_term = project_back(summed_t[:col_count], w_key) + project_back(
        summed_t[col_count:], w_value
    )
    result = head_sum(query_term + kv_term)
    return result


def solution(mesh):
    tm_size = mesh.shape["tm"]
    tensor_size = mesh.shape["tensor"]
    split = Mesh(mesh.devices.reshape(tm_size // 2, 2, tensor_size), ("tq", "zh", "tensor"))
    rows = P(("tq", "zh"), None)
    return jax.shard_map(
        local,
        mesh=split,
        in_specs=(
            rows,
            rows,
            P(None, "tensor"),
            P(None, "tensor"),
            P(None, "tensor"),
            P("tensor", None),
            P(),
        ),
        out_specs=rows,
        check_vma=False,
    )
```

```python
import jax
import jax.numpy as jnp
from jax import lax
from jax.sharding import Mesh, PartitionSpec as P

HD = 64
SPAN = 128


def attend_grad(query_t, key_t, value_t, dout_t):
    scaling = HD ** (-0.5)
    scores = (
        jnp.einsum("chdq,cjhdk->chqjk", query_t, key_t, preferred_element_type=jnp.float32)
        * scaling
    )
    probs = jax.nn.softmax(scores, axis=(-2, -1))
    probs_b = probs.astype(jnp.bfloat16)
    attn = jnp.einsum("chqjk,cjhdk->chdq", probs_b, value_t, preferred_element_type=jnp.float32)
    delta = jnp.sum(dout_t.astype(jnp.float32) * attn, axis=2)
    dprobs = jnp.einsum("chdq,cjhdk->chqjk", dout_t, value_t, preferred_element_type=jnp.float32)
    dscores_b = (probs * (dprobs - delta[:, :, :, None, None])).astype(jnp.bfloat16)
    grad_query = (
        jnp.einsum("chqjk,cjhdk->chdq", dscores_b, key_t, preferred_element_type=jnp.float32)
        * scaling
    ).astype(jnp.bfloat16)
    grad_key = (
        jnp.einsum("chqjk,chdq->cjhdk", dscores_b, query_t, preferred_element_type=jnp.float32)
        * scaling
    ).astype(jnp.bfloat16)
    grad_value = jnp.einsum(
        "chqjk,chdq->cjhdk", probs_b, dout_t, preferred_element_type=jnp.float32
    ).astype(jnp.bfloat16)
    return (grad_query, grad_key, grad_value)


def project_back(grads_t, weight):
    return lax.dot_general(
        grads_t, weight, (((0,), (1,)), ((), ())), preferred_element_type=jnp.float32
    )


def project_cols(weight, inputs):
    return lax.dot_general(
        weight, inputs, (((0,), (1,)), ((), ())), preferred_element_type=jnp.float32
    )


def head_sum(partial, chains=2):
    index = lax.axis_index("tensor")
    count = lax.axis_size("tensor")
    curs = jnp.split(partial, chains, axis=1)
    step = 1
    while step < count:
        upper = (index & step) != 0
        pairs = [(i, i ^ step) for i in range(count)]
        nxt = []
        for cur in curs:
            half = cur.shape[0] // 2
            low, high = cur[:half], cur[half:]
            keep = jnp.where(upper, high, low)
            send = jnp.where(upper, low, high)
            got = lax.ppermute(send.astype(jnp.bfloat16), "tensor", pairs)
            nxt.append(keep + got.astype(jnp.float32))
        curs = nxt
        step *= 2
    curs = [cur.astype(jnp.bfloat16) for cur in curs]
    while step > 1:
        step //= 2
        upper = (index & step) != 0
        pairs = [(i, i ^ step) for i in range(count)]
        nxt = []
        for cur in curs:
            got = lax.ppermute(cur, "tensor", pairs)
            nxt.append(jnp.where(upper, jnp.concatenate([got, cur]), jnp.concatenate([cur, got])))
        curs = nxt
    return jnp.concatenate(curs, axis=1).astype(jnp.float32)


def local(normed, grad_out, w_query, w_key, w_value, w_out, key_span):
    column_count = lax.axis_size("tq")
    side_count = lax.axis_size("zh")
    my_column = lax.axis_index("tq")
    my_side = lax.axis_index("zh")
    device_count = column_count * side_count
    my_index = my_column * side_count + my_side
    swap = [(0, 1), (1, 0)]
    row_count = normed.shape[0]
    col_count = w_query.shape[1]
    head_count = col_count // HD
    owned = row_count // SPAN
    per_reader = key_span.shape[1]
    queries_t = project_cols(w_query, normed).astype(jnp.bfloat16)
    keys_t = project_cols(w_key, normed).astype(jnp.bfloat16)
    values_t = project_cols(w_value, normed).astype(jnp.bfloat16)
    dout_t = lax.dot_general(
        w_out, grad_out, (((1,), (1,)), ((), ())), preferred_element_type=jnp.float32
    ).astype(jnp.bfloat16)
    paired_t = jnp.concatenate([keys_t, values_t], axis=0)
    paired_spans = jnp.transpose(paired_t.reshape(2 * col_count, owned, SPAN), (1, 0, 2))
    mirror_spans = lax.ppermute(paired_spans, "zh", swap)
    all_pairs = key_span.reshape(column_count, side_count, owned * per_reader)
    requests = lax.dynamic_index_in_dim(all_pairs, my_side, axis=1, keepdims=False)
    sides = my_column * side_count + jnp.arange(side_count, dtype=jnp.int32)
    hit = (requests // owned)[:, :, None] == sides[None, None, :]
    slot = jnp.sum(jnp.where(hit, (requests % owned)[:, :, None], 0), axis=1)
    exists = jnp.any(hit, axis=1)
    own_slot = lax.dynamic_index_in_dim(slot, my_side, axis=1, keepdims=False)
    mirror_slot = lax.dynamic_index_in_dim(slot, 1 - my_side, axis=1, keepdims=False)
    near = lax.all_to_all(paired_spans[own_slot], "tq", split_axis=0, concat_axis=0, tiled=True)
    far = lax.all_to_all(mirror_spans[mirror_slot], "tq", split_axis=0, concat_axis=0, tiled=True)
    incoming = jnp.where(
        my_side == 0, jnp.stack([near, far], axis=1), jnp.stack([far, near], axis=1)
    ).reshape(device_count, 2 * col_count, SPAN)
    own_ids = lax.dynamic_slice_in_dim(key_span, my_index * owned, owned, 0)
    owner_ids = (own_ids // owned).reshape(-1)
    fetched = incoming[owner_ids]
    fetched = fetched.reshape(owned, per_reader, 2, head_count, HD, SPAN)
    query_rows = jnp.transpose(queries_t.reshape(head_count, HD, owned, SPAN), (2, 0, 1, 3))
    dout_rows = jnp.transpose(dout_t.reshape(head_count, HD, owned, SPAN), (2, 0, 1, 3))
    grad_query, grad_key, grad_value = attend_grad(
        query_rows, fetched[:, :, 0], fetched[:, :, 1], dout_rows
    )
    grad_query_t = jnp.transpose(grad_query, (1, 2, 0, 3)).reshape(col_count, row_count)
    query_term = project_back(grad_query_t, w_query)
    pair_grads = jnp.concatenate(
        [
            grad_key.reshape(owned * per_reader, col_count, SPAN),
            grad_value.reshape(owned * per_reader, col_count, SPAN),
        ],
        axis=1,
    )
    returned = (
        jnp.zeros((device_count, 2 * col_count, SPAN), jnp.bfloat16).at[owner_ids].set(pair_grads)
    )
    returned = returned.reshape(column_count, side_count, 2 * col_count, SPAN)
    picked = (
        exists[:, :, None] & (slot[:, :, None] == jnp.arange(owned, dtype=jnp.int32)[None, None, :])
    ).astype(jnp.bfloat16)
    far_back = lax.all_to_all(
        lax.dynamic_index_in_dim(returned, 1 - my_side, axis=1, keepdims=False),
        "tq", split_axis=0, concat_axis=0, tiled=True,
    )
    other = jnp.einsum(
        "ck,crh->krh",
        lax.dynamic_index_in_dim(picked, 1 - my_side, axis=1, keepdims=False),
        far_back,
        preferred_element_type=jnp.float32,
    )
    other_back = lax.ppermute(other, "zh", swap)
    near_back = lax.all_to_all(
        lax.dynamic_index_in_dim(returned, my_side, axis=1, keepdims=False),
        "tq", split_axis=0, concat_axis=0, tiled=True,
    )
    mine = jnp.einsum(
        "ck,crh->krh",
        lax.dynamic_index_in_dim(picked, my_side, axis=1, keepdims=False),
        near_back,
        preferred_element_type=jnp.float32,
    )
    summed = (mine + other_back).astype(jnp.bfloat16)
    summed_t = jnp.transpose(summed, (1, 0, 2)).reshape(2 * col_count, row_count)
    kv_term = project_back(summed_t[:col_count], w_key) + project_back(
        summed_t[col_count:], w_value
    )
    result = head_sum(query_term + kv_term)
    return result


def solution(mesh):
    tm_size = mesh.shape["tm"]
    tensor_size = mesh.shape["tensor"]
    split = Mesh(mesh.devices.reshape(tm_size // 2, 2, tensor_size), ("tq", "zh", "tensor"))
    rows = P(("tq", "zh"), None)
    return jax.shard_map(
        local,
        mesh=split,
        in_specs=(
            rows,
            rows,
            P(None, "tensor"),
            P(None, "tensor"),
            P(None, "tensor"),
            P("tensor", None),
            P(),
        ),
        out_specs=rows,
        check_vma=False,
    )
```

```python
import jax
import jax.numpy as jnp
from jax import lax
from jax.sharding import Mesh, PartitionSpec as P

HD = 64
SPAN = 128


def attend_grad(query_t, key_t, value_t, dout_t):
    scaling = HD ** (-0.5)
    scores = (
        jnp.einsum("chdq,cjhdk->chqjk", query_t, key_t, preferred_element_type=jnp.float32)
        * scaling
    )
    probs = jax.nn.softmax(scores, axis=(-2, -1))
    probs_b = probs.astype(jnp.bfloat16)
    attn = jnp.einsum("chqjk,cjhdk->chdq", probs_b, value_t, preferred_element_type=jnp.float32)
    delta = jnp.sum(dout_t.astype(jnp.float32) * attn, axis=2)
    dprobs = jnp.einsum("chdq,cjhdk->chqjk", dout_t, value_t, preferred_element_type=jnp.float32)
    dscores_b = (probs * (dprobs - delta[:, :, :, None, None])).astype(jnp.bfloat16)
    grad_query = (
        jnp.einsum("chqjk,cjhdk->chdq", dscores_b, key_t, preferred_element_type=jnp.float32)
        * scaling
    ).astype(jnp.bfloat16)
    grad_key = (
        jnp.einsum("chqjk,chdq->cjhdk", dscores_b, query_t, preferred_element_type=jnp.float32)
        * scaling
    ).astype(jnp.bfloat16)
    grad_value = jnp.einsum(
        "chqjk,chdq->cjhdk", probs_b, dout_t, preferred_element_type=jnp.float32
    ).astype(jnp.bfloat16)
    return (grad_query, grad_key, grad_value)


def project_back(grads_t, weight):
    return lax.dot_general(
        grads_t, weight, (((0,), (1,)), ((), ())), preferred_element_type=jnp.float32
    )


def project_cols(weight, inputs):
    return lax.dot_general(
        weight, inputs, (((0,), (1,)), ((), ())), preferred_element_type=jnp.float32
    )


def head_sum(partial, radix=4):
    index = lax.axis_index("tensor")
    count = lax.axis_size("tensor")
    width = partial.shape[1]
    strides = []
    stride = 1
    while stride < count:
        strides.append(stride)
        stride *= radix

    def pairs(stride, flip):
        return [(i, i + ((((i // stride) % radix) ^ flip) - (i // stride) % radix) * stride) for i in range(count)]

    cur = partial
    for stride in strides:
        digit = (index // stride) % radix
        blocks = cur.reshape(radix, cur.shape[0] // radix, width)
        total = lax.dynamic_index_in_dim(blocks, digit, axis=0, keepdims=False)
        for flip in range(1, radix):
            send = lax.dynamic_index_in_dim(blocks, digit ^ flip, axis=0, keepdims=False)
            got = lax.ppermute(send.astype(jnp.bfloat16), "tensor", pairs(stride, flip))
            total = total + got.astype(jnp.float32)
        cur = total
    cur = cur.astype(jnp.bfloat16)
    for stride in reversed(strides):
        digit = (index // stride) % radix
        gots = [cur] + [lax.ppermute(cur, "tensor", pairs(stride, flip)) for flip in range(1, radix)]
        order = digit ^ jnp.arange(radix, dtype=digit.dtype)
        cur = jnp.take(jnp.stack(gots), order, axis=0).reshape(-1, width)
    return cur.astype(jnp.float32)


def local(normed, grad_out, w_query, w_key, w_value, w_out, key_span):
    column_count = lax.axis_size("tq")
    side_count = lax.axis_size("zh")
    my_column = lax.axis_index("tq")
    my_side = lax.axis_index("zh")
    device_count = column_count * side_count
    my_index = my_column * side_count + my_side
    swap = [(0, 1), (1, 0)]
    row_count = normed.shape[0]
    col_count = w_query.shape[1]
    head_count = col_count // HD
    owned = row_count // SPAN
    per_reader = key_span.shape[1]
    queries_t = project_cols(w_query, normed).astype(jnp.bfloat16)
    keys_t = project_cols(w_key, normed).astype(jnp.bfloat16)
    values_t = project_cols(w_value, normed).astype(jnp.bfloat16)
    dout_t = lax.dot_general(
        w_out, grad_out, (((1,), (1,)), ((), ())), preferred_element_type=jnp.float32
    ).astype(jnp.bfloat16)
    paired_t = jnp.concatenate([keys_t, values_t], axis=0)
    paired_spans = jnp.transpose(paired_t.reshape(2 * col_count, owned, SPAN), (1, 0, 2))
    mirror_spans = lax.ppermute(paired_spans, "zh", swap)
    all_pairs = key_span.reshape(column_count, side_count, owned * per_reader)
    requests = lax.dynamic_index_in_dim(all_pairs, my_side, axis=1, keepdims=False)
    sides = my_column * side_count + jnp.arange(side_count, dtype=jnp.int32)
    hit = (requests // owned)[:, :, None] == sides[None, None, :]
    slot = jnp.sum(jnp.where(hit, (requests % owned)[:, :, None], 0), axis=1)
    exists = jnp.any(hit, axis=1)
    own_slot = lax.dynamic_index_in_dim(slot, my_side, axis=1, keepdims=False)
    mirror_slot = lax.dynamic_index_in_dim(slot, 1 - my_side, axis=1, keepdims=False)
    near = lax.all_to_all(paired_spans[own_slot], "tq", split_axis=0, concat_axis=0, tiled=True)
    far = lax.all_to_all(mirror_spans[mirror_slot], "tq", split_axis=0, concat_axis=0, tiled=True)
    incoming = jnp.where(
        my_side == 0, jnp.stack([near, far], axis=1), jnp.stack([far, near], axis=1)
    ).reshape(device_count, 2 * col_count, SPAN)
    own_ids = lax.dynamic_slice_in_dim(key_span, my_index * owned, owned, 0)
    owner_ids = (own_ids // owned).reshape(-1)
    fetched = incoming[owner_ids]
    fetched = fetched.reshape(owned, per_reader, 2, head_count, HD, SPAN)
    query_rows = jnp.transpose(queries_t.reshape(head_count, HD, owned, SPAN), (2, 0, 1, 3))
    dout_rows = jnp.transpose(dout_t.reshape(head_count, HD, owned, SPAN), (2, 0, 1, 3))
    grad_query, grad_key, grad_value = attend_grad(
        query_rows, fetched[:, :, 0], fetched[:, :, 1], dout_rows
    )
    grad_query_t = jnp.transpose(grad_query, (1, 2, 0, 3)).reshape(col_count, row_count)
    query_term = project_back(grad_query_t, w_query)
    pair_grads = jnp.concatenate(
        [
            grad_key.reshape(owned * per_reader, col_count, SPAN),
            grad_value.reshape(owned * per_reader, col_count, SPAN),
        ],
        axis=1,
    )
    returned = (
        jnp.zeros((device_count, 2 * col_count, SPAN), jnp.bfloat16).at[owner_ids].set(pair_grads)
    )
    returned = returned.reshape(column_count, side_count, 2 * col_count, SPAN)
    picked = (
        exists[:, :, None] & (slot[:, :, None] == jnp.arange(owned, dtype=jnp.int32)[None, None, :])
    ).astype(jnp.bfloat16)
    far_back = lax.all_to_all(
        lax.dynamic_index_in_dim(returned, 1 - my_side, axis=1, keepdims=False),
        "tq", split_axis=0, concat_axis=0, tiled=True,
    )
    other = jnp.einsum(
        "ck,crh->krh",
        lax.dynamic_index_in_dim(picked, 1 - my_side, axis=1, keepdims=False),
        far_back,
        preferred_element_type=jnp.float32,
    )
    other_back = lax.ppermute(other, "zh", swap)
    near_back = lax.all_to_all(
        lax.dynamic_index_in_dim(returned, my_side, axis=1, keepdims=False),
        "tq", split_axis=0, concat_axis=0, tiled=True,
    )
    mine = jnp.einsum(
        "ck,crh->krh",
        lax.dynamic_index_in_dim(picked, my_side, axis=1, keepdims=False),
        near_back,
        preferred_element_type=jnp.float32,
    )
    summed = (mine + other_back).astype(jnp.bfloat16)
    summed_t = jnp.transpose(summed, (1, 0, 2)).reshape(2 * col_count, row_count)
    kv_term = project_back(summed_t[:col_count], w_key) + project_back(
        summed_t[col_count:], w_value
    )
    result = head_sum(query_term + kv_term)
    return result


def solution(mesh):
    tm_size = mesh.shape["tm"]
    tensor_size = mesh.shape["tensor"]
    split = Mesh(mesh.devices.reshape(tm_size // 2, 2, tensor_size), ("tq", "zh", "tensor"))
    rows = P(("tq", "zh"), None)
    return jax.shard_map(
        local,
        mesh=split,
        in_specs=(
            rows,
            rows,
            P(None, "tensor"),
            P(None, "tensor"),
            P(None, "tensor"),
            P("tensor", None),
            P(),
        ),
        out_specs=rows,
        check_vma=False,
    )
```

```python
import jax
import jax.numpy as jnp
from jax import lax
from jax.sharding import Mesh, PartitionSpec as P

HD = 64
SPAN = 128


def attend_grad(query_t, key_t, value_t, dout_t):
    scaling = HD ** (-0.5)
    scores = (
        jnp.einsum("chdq,cjhdk->chqjk", query_t, key_t, preferred_element_type=jnp.float32)
        * scaling
    )
    probs = jax.nn.softmax(scores, axis=(-2, -1))
    probs_b = probs.astype(jnp.bfloat16)
    attn = jnp.einsum("chqjk,cjhdk->chdq", probs_b, value_t, preferred_element_type=jnp.float32)
    delta = jnp.sum(dout_t.astype(jnp.float32) * attn, axis=2)
    dprobs = jnp.einsum("chdq,cjhdk->chqjk", dout_t, value_t, preferred_element_type=jnp.float32)
    dscores_b = (probs * (dprobs - delta[:, :, :, None, None])).astype(jnp.bfloat16)
    grad_query = (
        jnp.einsum("chqjk,cjhdk->chdq", dscores_b, key_t, preferred_element_type=jnp.float32)
        * scaling
    ).astype(jnp.bfloat16)
    grad_key = (
        jnp.einsum("chqjk,chdq->cjhdk", dscores_b, query_t, preferred_element_type=jnp.float32)
        * scaling
    ).astype(jnp.bfloat16)
    grad_value = jnp.einsum(
        "chqjk,chdq->cjhdk", probs_b, dout_t, preferred_element_type=jnp.float32
    ).astype(jnp.bfloat16)
    return (grad_query, grad_key, grad_value)


def project_back(grads_t, weight):
    return lax.dot_general(
        grads_t, weight, (((0,), (1,)), ((), ())), preferred_element_type=jnp.float32
    )


def project_cols(weight, inputs):
    return lax.dot_general(
        weight, inputs, (((0,), (1,)), ((), ())), preferred_element_type=jnp.float32
    )


def head_sum(partial):
    index = lax.axis_index("tensor")
    count = lax.axis_size("tensor")
    cur = partial
    step = 1
    while step < count:
        upper = (index & step) != 0
        half = cur.shape[0] // 2
        low, high = cur[:half], cur[half:]
        keep = jnp.where(upper, high, low)
        send = jnp.where(upper, low, high)
        got = lax.ppermute(send.astype(jnp.bfloat16), "tensor", [(i, i ^ step) for i in range(count)])
        cur = keep + got.astype(jnp.float32)
        step *= 2
    cur = cur.astype(jnp.bfloat16)
    while step > 1:
        step //= 2
        upper = (index & step) != 0
        got = lax.ppermute(cur, "tensor", [(i, i ^ step) for i in range(count)])
        cur = jnp.where(upper, jnp.concatenate([got, cur]), jnp.concatenate([cur, got]))
    return cur.astype(jnp.float32)


def local(normed, grad_out, w_query, w_key, w_value, w_out, key_span):
    column_count = lax.axis_size("tq")
    side_count = lax.axis_size("zh")
    my_column = lax.axis_index("tq")
    my_side = lax.axis_index("zh")
    device_count = column_count * side_count
    my_index = my_column * side_count + my_side
    swap = [(0, 1), (1, 0)]
    row_count = normed.shape[0]
    col_count = w_query.shape[1]
    head_count = col_count // HD
    owned = row_count // SPAN
    per_reader = key_span.shape[1]
    queries_t = project_cols(w_query, normed).astype(jnp.bfloat16)
    keys_t = project_cols(w_key, normed).astype(jnp.bfloat16)
    values_t = project_cols(w_value, normed).astype(jnp.bfloat16)
    dout_t = lax.dot_general(
        w_out, grad_out, (((1,), (1,)), ((), ())), preferred_element_type=jnp.float32
    ).astype(jnp.bfloat16)
    paired_t = jnp.concatenate([keys_t, values_t], axis=0)
    paired_spans = jnp.transpose(paired_t.reshape(2 * col_count, owned, SPAN), (1, 0, 2))
    mirror_spans = lax.ppermute(paired_spans, "zh", swap)
    all_pairs = key_span.reshape(column_count, side_count, owned * per_reader)
    requests = lax.dynamic_index_in_dim(all_pairs, my_side, axis=1, keepdims=False)
    sides = my_column * side_count + jnp.arange(side_count, dtype=jnp.int32)
    hit = (requests // owned)[:, :, None] == sides[None, None, :]
    slot = jnp.sum(jnp.where(hit, (requests % owned)[:, :, None], 0), axis=1)
    exists = jnp.any(hit, axis=1)
    own_slot = lax.dynamic_index_in_dim(slot, my_side, axis=1, keepdims=False)
    mirror_slot = lax.dynamic_index_in_dim(slot, 1 - my_side, axis=1, keepdims=False)
    near = lax.all_to_all(paired_spans[own_slot], "tq", split_axis=0, concat_axis=0, tiled=True)
    far = lax.all_to_all(mirror_spans[mirror_slot], "tq", split_axis=0, concat_axis=0, tiled=True)
    own_ids = lax.dynamic_slice_in_dim(key_span, my_index * owned, owned, 0)
    owner_ids = (own_ids // owned).reshape(-1)
    owner_column = owner_ids // side_count
    from_near = owner_ids % side_count == my_side
    fetched = jnp.where(from_near[:, None, None], near[owner_column], far[owner_column])
    fetched = fetched.reshape(owned, per_reader, 2, head_count, HD, SPAN)
    query_rows = jnp.transpose(queries_t.reshape(head_count, HD, owned, SPAN), (2, 0, 1, 3))
    dout_rows = jnp.transpose(dout_t.reshape(head_count, HD, owned, SPAN), (2, 0, 1, 3))
    grad_query, grad_key, grad_value = attend_grad(
        query_rows, fetched[:, :, 0], fetched[:, :, 1], dout_rows
    )
    grad_query_t = jnp.transpose(grad_query, (1, 2, 0, 3)).reshape(col_count, row_count)
    query_term = project_back(grad_query_t, w_query)
    pair_grads = jnp.concatenate(
        [
            grad_key.reshape(owned * per_reader, col_count, SPAN),
            grad_value.reshape(owned * per_reader, col_count, SPAN),
        ],
        axis=1,
    )
    pair_count = owned * per_reader
    pair_index = jnp.arange(pair_count, dtype=jnp.int32)
    unused = jnp.full((column_count,), pair_count, jnp.int32)
    near_pair = unused.at[jnp.where(from_near, owner_column, column_count)].set(pair_index, mode="drop")
    far_pair = unused.at[jnp.where(from_near, column_count, owner_column)].set(pair_index, mode="drop")
    picked = (
        exists[:, :, None] & (slot[:, :, None] == jnp.arange(owned, dtype=jnp.int32)[None, None, :])
    ).astype(jnp.bfloat16)
    far_back = lax.all_to_all(
        jnp.take(pair_grads, far_pair, axis=0, mode="fill", fill_value=0),
        "tq", split_axis=0, concat_axis=0, tiled=True,
    )
    other = jnp.einsum(
        "ck,crh->krh",
        lax.dynamic_index_in_dim(picked, 1 - my_side, axis=1, keepdims=False),
        far_back,
        preferred_element_type=jnp.float32,
    )
    other_back = lax.ppermute(other, "zh", swap)
    near_back = lax.all_to_all(
        jnp.take(pair_grads, near_pair, axis=0, mode="fill", fill_value=0),
        "tq", split_axis=0, concat_axis=0, tiled=True,
    )
    mine = jnp.einsum(
        "ck,crh->krh",
        lax.dynamic_index_in_dim(picked, my_side, axis=1, keepdims=False),
        near_back,
        preferred_element_type=jnp.float32,
    )
    summed = (mine + other_back).astype(jnp.bfloat16)
    summed_t = jnp.transpose(summed, (1, 0, 2)).reshape(2 * col_count, row_count)
    kv_term = project_back(summed_t[:col_count], w_key) + project_back(
        summed_t[col_count:], w_value
    )
    result = head_sum(query_term + kv_term)
    return result


def solution(mesh):
    tm_size = mesh.shape["tm"]
    tensor_size = mesh.shape["tensor"]
    split = Mesh(mesh.devices.reshape(tm_size // 2, 2, tensor_size), ("tq", "zh", "tensor"))
    rows = P(("tq", "zh"), None)
    return jax.shard_map(
        local,
        mesh=split,
        in_specs=(
            rows,
            rows,
            P(None, "tensor"),
            P(None, "tensor"),
            P(None, "tensor"),
            P("tensor", None),
            P(),
        ),
        out_specs=rows,
        check_vma=False,
    )
```

```python
import jax
import jax.numpy as jnp
from jax import lax
from jax.sharding import Mesh, PartitionSpec as P

HD = 64
SPAN = 128


def attend_grad(query_t, key_t, value_t, dout_t):
    scaling = HD ** (-0.5)
    scores = (
        jnp.einsum("chdq,cjhdk->chqjk", query_t, key_t, preferred_element_type=jnp.float32)
        * scaling
    )
    probs = jax.nn.softmax(scores, axis=(-2, -1))
    probs_b = probs.astype(jnp.bfloat16)
    attn = jnp.einsum("chqjk,cjhdk->chdq", probs_b, value_t, preferred_element_type=jnp.float32)
    delta = jnp.sum(dout_t.astype(jnp.float32) * attn, axis=2)
    dprobs = jnp.einsum("chdq,cjhdk->chqjk", dout_t, value_t, preferred_element_type=jnp.float32)
    dscores_b = (probs * (dprobs - delta[:, :, :, None, None])).astype(jnp.bfloat16)
    grad_query = (
        jnp.einsum("chqjk,cjhdk->chdq", dscores_b, key_t, preferred_element_type=jnp.float32)
        * scaling
    ).astype(jnp.bfloat16)
    grad_key = (
        jnp.einsum("chqjk,chdq->cjhdk", dscores_b, query_t, preferred_element_type=jnp.float32)
        * scaling
    ).astype(jnp.bfloat16)
    grad_value = jnp.einsum(
        "chqjk,chdq->cjhdk", probs_b, dout_t, preferred_element_type=jnp.float32
    ).astype(jnp.bfloat16)
    return (grad_query, grad_key, grad_value)


def project_back(grads_t, weight):
    return lax.dot_general(
        grads_t, weight, (((0,), (1,)), ((), ())), preferred_element_type=jnp.float32
    )


def project_cols(weight, inputs):
    return lax.dot_general(
        weight, inputs, (((0,), (1,)), ((), ())), preferred_element_type=jnp.float32
    )


def head_sum(partial):
    index = lax.axis_index("tensor")
    count = lax.axis_size("tensor")
    cur = partial
    step = 1
    while step < count:
        upper = (index & step) != 0
        half = cur.shape[0] // 2
        low, high = cur[:half], cur[half:]
        keep = jnp.where(upper, high, low)
        send = jnp.where(upper, low, high)
        got = lax.ppermute(send.astype(jnp.bfloat16), "tensor", [(i, i ^ step) for i in range(count)])
        cur = keep + got.astype(jnp.float32)
        step *= 2
    cur = cur.astype(jnp.bfloat16)
    while step > 1:
        step //= 2
        upper = (index & step) != 0
        got = lax.ppermute(cur, "tensor", [(i, i ^ step) for i in range(count)])
        cur = jnp.where(upper, jnp.concatenate([got, cur]), jnp.concatenate([cur, got]))
    return cur.astype(jnp.float32)


def relay_pairs(side_count, tensor_count, hop):
    line = tensor_count // 2
    ring = side_count * line
    pairs = []
    for side in range(side_count):
        for t in range(tensor_count):
            z = (side * line + t // 2 + hop) % ring
            pairs.append((side * tensor_count + t, (z // line) * tensor_count + (z % line) * 2 + t % 2))
    return pairs


def mirror_swap(payload):
    side_count = lax.axis_size("zh")
    tensor_count = lax.axis_size("tensor")
    quarter = tensor_count // 2 * side_count // 4
    ahead, behind = jnp.split(payload, 2, axis=0)
    for _ in range(2):
        ahead = lax.ppermute(ahead, ("zh", "tensor"), relay_pairs(side_count, tensor_count, quarter))
        behind = lax.ppermute(behind, ("zh", "tensor"), relay_pairs(side_count, tensor_count, -quarter))
    return jnp.concatenate([ahead, behind], axis=0)


def local(normed, grad_out, w_query, w_key, w_value, w_out, key_span):
    column_count = lax.axis_size("tq")
    side_count = lax.axis_size("zh")
    my_column = lax.axis_index("tq")
    my_side = lax.axis_index("zh")
    device_count = column_count * side_count
    my_index = my_column * side_count + my_side
    swap = [(0, 1), (1, 0)]
    row_count = normed.shape[0]
    col_count = w_query.shape[1]
    head_count = col_count // HD
    owned = row_count // SPAN
    per_reader = key_span.shape[1]
    queries_t = project_cols(w_query, normed).astype(jnp.bfloat16)
    keys_t = project_cols(w_key, normed).astype(jnp.bfloat16)
    values_t = project_cols(w_value, normed).astype(jnp.bfloat16)
    dout_t = lax.dot_general(
        w_out, grad_out, (((1,), (1,)), ((), ())), preferred_element_type=jnp.float32
    ).astype(jnp.bfloat16)
    paired_t = jnp.concatenate([keys_t, values_t], axis=0)
    paired_spans = jnp.transpose(paired_t.reshape(2 * col_count, owned, SPAN), (1, 0, 2))
    mirror_spans = lax.ppermute(paired_spans, "zh", swap)
    all_pairs = key_span.reshape(column_count, side_count, owned * per_reader)
    requests = lax.dynamic_index_in_dim(all_pairs, my_side, axis=1, keepdims=False)
    sides = my_column * side_count + jnp.arange(side_count, dtype=jnp.int32)
    hit = (requests // owned)[:, :, None] == sides[None, None, :]
    slot = jnp.sum(jnp.where(hit, (requests % owned)[:, :, None], 0), axis=1)
    exists = jnp.any(hit, axis=1)
    own_slot = lax.dynamic_index_in_dim(slot, my_side, axis=1, keepdims=False)
    mirror_slot = lax.dynamic_index_in_dim(slot, 1 - my_side, axis=1, keepdims=False)
    near = lax.all_to_all(paired_spans[own_slot], "tq", split_axis=0, concat_axis=0, tiled=True)
    far = lax.all_to_all(mirror_spans[mirror_slot], "tq", split_axis=0, concat_axis=0, tiled=True)
    own_ids = lax.dynamic_slice_in_dim(key_span, my_index * owned, owned, 0)
    owner_ids = (own_ids // owned).reshape(-1)
    owner_column = owner_ids // side_count
    from_near = owner_ids % side_count == my_side
    fetched = jnp.where(from_near[:, None, None], near[owner_column], far[owner_column])
    fetched = fetched.reshape(owned, per_reader, 2, head_count, HD, SPAN)
    query_rows = jnp.transpose(queries_t.reshape(head_count, HD, owned, SPAN), (2, 0, 1, 3))
    dout_rows = jnp.transpose(dout_t.reshape(head_count, HD, owned, SPAN), (2, 0, 1, 3))
    grad_query, grad_key, grad_value = attend_grad(
        query_rows, fetched[:, :, 0], fetched[:, :, 1], dout_rows
    )
    grad_query_t = jnp.transpose(grad_query, (1, 2, 0, 3)).reshape(col_count, row_count)
    query_term = project_back(grad_query_t, w_query)
    pair_grads = jnp.concatenate(
        [
            grad_key.reshape(owned * per_reader, col_count, SPAN),
            grad_value.reshape(owned * per_reader, col_count, SPAN),
        ],
        axis=1,
    )
    pair_count = owned * per_reader
    pair_index = jnp.arange(pair_count, dtype=jnp.int32)
    unused = jnp.full((column_count,), pair_count, jnp.int32)
    near_pair = unused.at[jnp.where(from_near, owner_column, column_count)].set(pair_index, mode="drop")
    far_pair = unused.at[jnp.where(from_near, column_count, owner_column)].set(pair_index, mode="drop")
    picked = (
        exists[:, :, None] & (slot[:, :, None] == jnp.arange(owned, dtype=jnp.int32)[None, None, :])
    ).astype(jnp.bfloat16)
    far_back = lax.all_to_all(
        jnp.take(pair_grads, far_pair, axis=0, mode="fill", fill_value=0),
        "tq", split_axis=0, concat_axis=0, tiled=True,
    )
    other = jnp.einsum(
        "ck,crh->krh",
        lax.dynamic_index_in_dim(picked, 1 - my_side, axis=1, keepdims=False),
        far_back,
        preferred_element_type=jnp.float32,
    )
    other_back = mirror_swap(other)
    near_back = lax.all_to_all(
        jnp.take(pair_grads, near_pair, axis=0, mode="fill", fill_value=0),
        "tq", split_axis=0, concat_axis=0, tiled=True,
    )
    mine = jnp.einsum(
        "ck,crh->krh",
        lax.dynamic_index_in_dim(picked, my_side, axis=1, keepdims=False),
        near_back,
        preferred_element_type=jnp.float32,
    )
    summed = (mine + other_back).astype(jnp.bfloat16)
    summed_t = jnp.transpose(summed, (1, 0, 2)).reshape(2 * col_count, row_count)
    kv_term = project_back(summed_t[:col_count], w_key) + project_back(
        summed_t[col_count:], w_value
    )
    result = head_sum(query_term + kv_term)
    return result


def solution(mesh):
    tm_size = mesh.shape["tm"]
    tensor_size = mesh.shape["tensor"]
    split = Mesh(mesh.devices.reshape(tm_size // 2, 2, tensor_size), ("tq", "zh", "tensor"))
    rows = P(("tq", "zh"), None)
    return jax.shard_map(
        local,
        mesh=split,
        in_specs=(
            rows,
            rows,
            P(None, "tensor"),
            P(None, "tensor"),
            P(None, "tensor"),
            P("tensor", None),
            P(),
        ),
        out_specs=rows,
        check_vma=False,
    )
```

```python
import jax
import jax.numpy as jnp
from jax import lax
from jax.sharding import Mesh, PartitionSpec as P

HD = 64
SPAN = 128


def attend_grad(query_t, key_t, value_t, dout_t):
    scaling = HD ** (-0.5)
    scores = (
        jnp.einsum("chdq,cjhdk->chqjk", query_t, key_t, preferred_element_type=jnp.float32)
        * scaling
    )
    probs = jax.nn.softmax(scores, axis=(-2, -1))
    probs_b = probs.astype(jnp.bfloat16)
    attn = jnp.einsum("chqjk,cjhdk->chdq", probs_b, value_t, preferred_element_type=jnp.float32)
    delta = jnp.sum(dout_t.astype(jnp.float32) * attn, axis=2)
    dprobs = jnp.einsum("chdq,cjhdk->chqjk", dout_t, value_t, preferred_element_type=jnp.float32)
    dscores_b = (probs * (dprobs - delta[:, :, :, None, None])).astype(jnp.bfloat16)
    grad_query = (
        jnp.einsum("chqjk,cjhdk->chdq", dscores_b, key_t, preferred_element_type=jnp.float32)
        * scaling
    ).astype(jnp.bfloat16)
    grad_key = (
        jnp.einsum("chqjk,chdq->cjhdk", dscores_b, query_t, preferred_element_type=jnp.float32)
        * scaling
    ).astype(jnp.bfloat16)
    grad_value = jnp.einsum(
        "chqjk,chdq->cjhdk", probs_b, dout_t, preferred_element_type=jnp.float32
    ).astype(jnp.bfloat16)
    return (grad_query, grad_key, grad_value)


def project_back(grads_t, weight):
    return lax.dot_general(
        grads_t, weight, (((0,), (1,)), ((), ())), preferred_element_type=jnp.float32
    )


def project_cols(weight, inputs):
    return lax.dot_general(
        weight, inputs, (((0,), (1,)), ((), ())), preferred_element_type=jnp.float32
    )


def head_sum(partial):
    index = lax.axis_index("tensor")
    count = lax.axis_size("tensor")
    cur = partial
    step = 1
    while step < count:
        upper = (index & step) != 0
        half = cur.shape[0] // 2
        low, high = cur[:half], cur[half:]
        keep = jnp.where(upper, high, low)
        send = jnp.where(upper, low, high)
        got = lax.ppermute(send.astype(jnp.bfloat16), "tensor", [(i, i ^ step) for i in range(count)])
        cur = keep + got.astype(jnp.float32)
        step *= 2
    cur = cur.astype(jnp.bfloat16)
    while step > 1:
        step //= 2
        upper = (index & step) != 0
        got = lax.ppermute(cur, "tensor", [(i, i ^ step) for i in range(count)])
        cur = jnp.where(upper, jnp.concatenate([got, cur]), jnp.concatenate([cur, got]))
    return cur.astype(jnp.float32)


def local(normed, grad_out, w_query, w_key, w_value, w_out, key_span):
    column_count = lax.axis_size("tq")
    side_count = lax.axis_size("zh")
    my_column = lax.axis_index("tq")
    my_side = lax.axis_index("zh")
    device_count = column_count * side_count
    my_index = my_column * side_count + my_side
    swap = [(0, 1), (1, 0)]
    row_count = normed.shape[0]
    col_count = w_query.shape[1]
    head_count = col_count // HD
    owned = row_count // SPAN
    per_reader = key_span.shape[1]
    queries_t = project_cols(w_query, normed).astype(jnp.bfloat16)
    keys_t = project_cols(w_key, normed).astype(jnp.bfloat16)
    values_t = project_cols(w_value, normed).astype(jnp.bfloat16)
    dout_t = lax.dot_general(
        w_out, grad_out, (((1,), (1,)), ((), ())), preferred_element_type=jnp.float32
    ).astype(jnp.bfloat16)
    paired_t = jnp.concatenate([keys_t, values_t], axis=0)
    paired_spans = jnp.transpose(paired_t.reshape(2 * col_count, owned, SPAN), (1, 0, 2))
    mirror_spans = lax.ppermute(paired_spans, "zh", swap)
    all_pairs = key_span.reshape(column_count, side_count, owned * per_reader)
    requests = lax.dynamic_index_in_dim(all_pairs, my_side, axis=1, keepdims=False)
    sides = my_column * side_count + jnp.arange(side_count, dtype=jnp.int32)
    hit = (requests // owned)[:, :, None] == sides[None, None, :]
    slot = jnp.sum(jnp.where(hit, (requests % owned)[:, :, None], 0), axis=1)
    exists = jnp.any(hit, axis=1)
    own_slot = lax.dynamic_index_in_dim(slot, my_side, axis=1, keepdims=False)
    mirror_slot = lax.dynamic_index_in_dim(slot, 1 - my_side, axis=1, keepdims=False)
    near = lax.all_to_all(paired_spans[own_slot], "tq", split_axis=0, concat_axis=0, tiled=True)
    far = lax.all_to_all(mirror_spans[mirror_slot], "tq", split_axis=0, concat_axis=0, tiled=True)
    own_ids = lax.dynamic_slice_in_dim(key_span, my_index * owned, owned, 0)
    owner_ids = (own_ids // owned).reshape(-1)
    owner_column = owner_ids // side_count
    from_near = owner_ids % side_count == my_side
    fetched = jnp.where(from_near[:, None, None], near[owner_column], far[owner_column])
    fetched = fetched.reshape(owned, per_reader, 2, head_count, HD, SPAN)
    query_rows = jnp.transpose(queries_t.reshape(head_count, HD, owned, SPAN), (2, 0, 1, 3))
    dout_rows = jnp.transpose(dout_t.reshape(head_count, HD, owned, SPAN), (2, 0, 1, 3))
    grad_query, grad_key, grad_value = attend_grad(
        query_rows, fetched[:, :, 0], fetched[:, :, 1], dout_rows
    )
    grad_query_t = jnp.transpose(grad_query, (1, 2, 0, 3)).reshape(col_count, row_count)
    query_term = project_back(grad_query_t, w_query)
    pair_grads = jnp.concatenate(
        [
            grad_key.reshape(owned * per_reader, col_count, SPAN),
            grad_value.reshape(owned * per_reader, col_count, SPAN),
        ],
        axis=1,
    )
    pair_count = owned * per_reader
    pair_index = jnp.arange(pair_count, dtype=jnp.int32)
    unused = jnp.full((column_count,), pair_count, jnp.int32)
    near_pair = unused.at[jnp.where(from_near, owner_column, column_count)].set(pair_index, mode="drop")
    far_pair = unused.at[jnp.where(from_near, column_count, owner_column)].set(pair_index, mode="drop")
    picked = (
        exists[:, :, None] & (slot[:, :, None] == jnp.arange(owned, dtype=jnp.int32)[None, None, :])
    ).astype(jnp.bfloat16)
    far_back = lax.all_to_all(
        jnp.take(pair_grads, far_pair, axis=0, mode="fill", fill_value=0),
        "tq", split_axis=0, concat_axis=0, tiled=True,
    )
    other = jnp.einsum(
        "ck,crh->krh",
        lax.dynamic_index_in_dim(picked, 1 - my_side, axis=1, keepdims=False),
        far_back,
        preferred_element_type=jnp.float32,
    )
    other_back = lax.ppermute(other.astype(jnp.bfloat16), "zh", swap).astype(jnp.float32)
    near_back = lax.all_to_all(
        jnp.take(pair_grads, near_pair, axis=0, mode="fill", fill_value=0),
        "tq", split_axis=0, concat_axis=0, tiled=True,
    )
    mine = jnp.einsum(
        "ck,crh->krh",
        lax.dynamic_index_in_dim(picked, my_side, axis=1, keepdims=False),
        near_back,
        preferred_element_type=jnp.float32,
    )
    summed = (mine + other_back).astype(jnp.bfloat16)
    summed_t = jnp.transpose(summed, (1, 0, 2)).reshape(2 * col_count, row_count)
    kv_term = project_back(summed_t[:col_count], w_key) + project_back(
        summed_t[col_count:], w_value
    )
    result = head_sum(query_term + kv_term)
    return result


def solution(mesh):
    tm_size = mesh.shape["tm"]
    tensor_size = mesh.shape["tensor"]
    split = Mesh(mesh.devices.reshape(tm_size // 2, 2, tensor_size), ("tq", "zh", "tensor"))
    rows = P(("tq", "zh"), None)
    return jax.shard_map(
        local,
        mesh=split,
        in_specs=(
            rows,
            rows,
            P(None, "tensor"),
            P(None, "tensor"),
            P(None, "tensor"),
            P("tensor", None),
            P(),
        ),
        out_specs=rows,
        check_vma=False,
    )
```

```python
import jax
import jax.numpy as jnp
from jax import lax
from jax.sharding import Mesh, PartitionSpec as P

HD = 64
SPAN = 128


def attend_grad(query_t, key_t, value_t, dout_t):
    scaling = HD ** (-0.5)
    scores = (
        jnp.einsum("chdq,cjhdk->chqjk", query_t, key_t, preferred_element_type=jnp.float32)
        * scaling
    )
    probs = jax.nn.softmax(scores, axis=(-2, -1))
    probs_b = probs.astype(jnp.bfloat16)
    attn = jnp.einsum("chqjk,cjhdk->chdq", probs_b, value_t, preferred_element_type=jnp.float32)
    delta = jnp.sum(dout_t.astype(jnp.float32) * attn, axis=2)
    dprobs = jnp.einsum("chdq,cjhdk->chqjk", dout_t, value_t, preferred_element_type=jnp.float32)
    dscores_b = (probs * (dprobs - delta[:, :, :, None, None])).astype(jnp.bfloat16)
    grad_query = (
        jnp.einsum("chqjk,cjhdk->chdq", dscores_b, key_t, preferred_element_type=jnp.float32)
        * scaling
    ).astype(jnp.bfloat16)
    grad_key = (
        jnp.einsum("chqjk,chdq->cjhdk", dscores_b, query_t, preferred_element_type=jnp.float32)
        * scaling
    ).astype(jnp.bfloat16)
    grad_value = jnp.einsum(
        "chqjk,chdq->cjhdk", probs_b, dout_t, preferred_element_type=jnp.float32
    ).astype(jnp.bfloat16)
    return (grad_query, grad_key, grad_value)


def project_back(grads_t, weight):
    return lax.dot_general(
        grads_t, weight, (((0,), (1,)), ((), ())), preferred_element_type=jnp.float32
    )


def project_cols(weight, inputs):
    return lax.dot_general(
        weight, inputs, (((0,), (1,)), ((), ())), preferred_element_type=jnp.float32
    )


def head_sum(partial):
    index = lax.axis_index("tensor")
    count = lax.axis_size("tensor")
    cur = partial
    step = 1
    while step < count:
        upper = (index & step) != 0
        half = cur.shape[0] // 2
        low, high = cur[:half], cur[half:]
        keep = jnp.where(upper, high, low)
        send = jnp.where(upper, low, high)
        got = lax.ppermute(send.astype(jnp.bfloat16), "tensor", [(i, i ^ step) for i in range(count)])
        cur = keep + got.astype(jnp.float32)
        step *= 2
    cur = cur.astype(jnp.bfloat16)
    while step > 1:
        step //= 2
        upper = (index & step) != 0
        got = lax.ppermute(cur, "tensor", [(i, i ^ step) for i in range(count)])
        cur = jnp.where(upper, jnp.concatenate([got, cur]), jnp.concatenate([cur, got]))
    return cur.astype(jnp.float32)


def local(normed, grad_out, w_query, w_key, w_value, w_out, key_span):
    column_count = lax.axis_size("tq")
    side_count = lax.axis_size("zh")
    my_column = lax.axis_index("tq")
    my_side = lax.axis_index("zh")
    device_count = column_count * side_count
    my_index = my_column * side_count + my_side
    swap = [(0, 1), (1, 0)]
    row_count = normed.shape[0]
    col_count = w_query.shape[1]
    head_count = col_count // HD
    owned = row_count // SPAN
    per_reader = key_span.shape[1]
    queries_t = project_cols(w_query, normed).astype(jnp.bfloat16)
    keys_t = project_cols(w_key, normed).astype(jnp.bfloat16)
    values_t = project_cols(w_value, normed).astype(jnp.bfloat16)
    dout_t = lax.dot_general(
        w_out, grad_out, (((1,), (1,)), ((), ())), preferred_element_type=jnp.float32
    ).astype(jnp.bfloat16)
    paired_t = jnp.concatenate([keys_t, values_t], axis=0)
    paired_spans = jnp.transpose(paired_t.reshape(2 * col_count, owned, SPAN), (1, 0, 2))
    mirror_spans = lax.ppermute(paired_spans, "zh", swap)
    all_pairs = key_span.reshape(column_count, side_count, owned * per_reader)
    requests = lax.dynamic_index_in_dim(all_pairs, my_side, axis=1, keepdims=False)
    sides = my_column * side_count + jnp.arange(side_count, dtype=jnp.int32)
    hit = (requests // owned)[:, :, None] == sides[None, None, :]
    slot = jnp.sum(jnp.where(hit, (requests % owned)[:, :, None], 0), axis=1)
    exists = jnp.any(hit, axis=1)
    own_slot = lax.dynamic_index_in_dim(slot, my_side, axis=1, keepdims=False)
    mirror_slot = lax.dynamic_index_in_dim(slot, 1 - my_side, axis=1, keepdims=False)
    near = lax.all_to_all(paired_spans[own_slot], "tq", split_axis=0, concat_axis=0, tiled=True)
    far = lax.all_to_all(mirror_spans[mirror_slot], "tq", split_axis=0, concat_axis=0, tiled=True)
    own_ids = lax.dynamic_slice_in_dim(key_span, my_index * owned, owned, 0)
    owner_ids = (own_ids // owned).reshape(-1)
    owner_column = owner_ids // side_count
    from_near = owner_ids % side_count == my_side
    fetched = jnp.where(from_near[:, None, None], near[owner_column], far[owner_column])
    fetched = fetched.reshape(owned, per_reader, 2, head_count, HD, SPAN)
    query_rows = jnp.transpose(queries_t.reshape(head_count, HD, owned, SPAN), (2, 0, 1, 3))
    dout_rows = jnp.transpose(dout_t.reshape(head_count, HD, owned, SPAN), (2, 0, 1, 3))
    grad_query, grad_key, grad_value = attend_grad(
        query_rows, fetched[:, :, 0], fetched[:, :, 1], dout_rows
    )
    grad_query_t = jnp.transpose(grad_query, (1, 2, 0, 3)).reshape(col_count, row_count)
    query_term = project_back(grad_query_t, w_query)
    pair_grads = jnp.concatenate(
        [
            grad_key.reshape(owned * per_reader, col_count, SPAN),
            grad_value.reshape(owned * per_reader, col_count, SPAN),
        ],
        axis=1,
    )
    pair_count = owned * per_reader
    pair_index = jnp.arange(pair_count, dtype=jnp.int32)
    unused = jnp.full((column_count,), pair_count, jnp.int32)
    near_pair = unused.at[jnp.where(from_near, owner_column, column_count)].set(pair_index, mode="drop")
    far_pair = unused.at[jnp.where(from_near, column_count, owner_column)].set(pair_index, mode="drop")
    picked = (
        exists[:, :, None] & (slot[:, :, None] == jnp.arange(owned, dtype=jnp.int32)[None, None, :])
    ).astype(jnp.bfloat16)
    far_back = lax.all_to_all(
        jnp.take(pair_grads, far_pair, axis=0, mode="clip"),
        "tq", split_axis=0, concat_axis=0, tiled=True,
    )
    other = jnp.einsum(
        "ck,crh->krh",
        lax.dynamic_index_in_dim(picked, 1 - my_side, axis=1, keepdims=False),
        far_back,
        preferred_element_type=jnp.float32,
    )
    other_back = lax.ppermute(other, "zh", swap)
    near_back = lax.all_to_all(
        jnp.take(pair_grads, near_pair, axis=0, mode="clip"),
        "tq", split_axis=0, concat_axis=0, tiled=True,
    )
    mine = jnp.einsum(
        "ck,crh->krh",
        lax.dynamic_index_in_dim(picked, my_side, axis=1, keepdims=False),
        near_back,
        preferred_element_type=jnp.float32,
    )
    summed = (mine + other_back).astype(jnp.bfloat16)
    summed_t = jnp.transpose(summed, (1, 0, 2)).reshape(2 * col_count, row_count)
    kv_term = project_back(summed_t[:col_count], w_key) + project_back(
        summed_t[col_count:], w_value
    )
    result = head_sum(query_term + kv_term)
    return result


def solution(mesh):
    tm_size = mesh.shape["tm"]
    tensor_size = mesh.shape["tensor"]
    split = Mesh(mesh.devices.reshape(tm_size // 2, 2, tensor_size), ("tq", "zh", "tensor"))
    rows = P(("tq", "zh"), None)
    return jax.shard_map(
        local,
        mesh=split,
        in_specs=(
            rows,
            rows,
            P(None, "tensor"),
            P(None, "tensor"),
            P(None, "tensor"),
            P("tensor", None),
            P(),
        ),
        out_specs=rows,
        check_vma=False,
    )
```

```python
import jax
import jax.numpy as jnp
from jax import lax
from jax.sharding import Mesh, PartitionSpec as P

HD = 64
SPAN = 128


def attend_grad(query_t, key_t, value_t, dout_t):
    scaling = HD ** (-0.5)
    scores = (
        jnp.einsum("chdq,cjhdk->chqjk", query_t, key_t, preferred_element_type=jnp.float32)
        * scaling
    )
    probs = jax.nn.softmax(scores, axis=(-2, -1))
    probs_b = probs.astype(jnp.bfloat16)
    attn = jnp.einsum("chqjk,cjhdk->chdq", probs_b, value_t, preferred_element_type=jnp.float32)
    delta = jnp.sum(dout_t.astype(jnp.float32) * attn, axis=2)
    dprobs = jnp.einsum("chdq,cjhdk->chqjk", dout_t, value_t, preferred_element_type=jnp.float32)
    dscores_b = (probs * (dprobs - delta[:, :, :, None, None])).astype(jnp.bfloat16)
    grad_query = (
        jnp.einsum("chqjk,cjhdk->chdq", dscores_b, key_t, preferred_element_type=jnp.float32)
        * scaling
    ).astype(jnp.bfloat16)
    grad_pair = jnp.einsum(
        "gchqjk,gchdq->cjghdk",
        jnp.stack([dscores_b, probs_b]),
        jnp.stack([query_t * scaling, dout_t]),
        preferred_element_type=jnp.float32,
    ).astype(jnp.bfloat16)
    return (grad_query, grad_pair)


def project_back(grads_t, weight):
    return lax.dot_general(
        grads_t, weight, (((0,), (1,)), ((), ())), preferred_element_type=jnp.float32
    )


def project_cols(weight, inputs):
    return lax.dot_general(
        weight, inputs, (((0,), (1,)), ((), ())), preferred_element_type=jnp.float32
    )


def head_sum(partial):
    index = lax.axis_index("tensor")
    count = lax.axis_size("tensor")
    cur = partial
    step = 1
    while step < count:
        upper = (index & step) != 0
        half = cur.shape[0] // 2
        low, high = cur[:half], cur[half:]
        keep = jnp.where(upper, high, low)
        send = jnp.where(upper, low, high)
        got = lax.ppermute(send.astype(jnp.bfloat16), "tensor", [(i, i ^ step) for i in range(count)])
        cur = keep + got.astype(jnp.float32)
        step *= 2
    cur = cur.astype(jnp.bfloat16)
    while step > 1:
        step //= 2
        upper = (index & step) != 0
        got = lax.ppermute(cur, "tensor", [(i, i ^ step) for i in range(count)])
        cur = jnp.where(upper, jnp.concatenate([got, cur]), jnp.concatenate([cur, got]))
    return cur.astype(jnp.float32)


def local(normed, grad_out, w_query, w_key, w_value, w_out, key_span):
    column_count = lax.axis_size("tq")
    side_count = lax.axis_size("zh")
    my_column = lax.axis_index("tq")
    my_side = lax.axis_index("zh")
    device_count = column_count * side_count
    my_index = my_column * side_count + my_side
    swap = [(0, 1), (1, 0)]
    row_count = normed.shape[0]
    col_count = w_query.shape[1]
    head_count = col_count // HD
    owned = row_count // SPAN
    per_reader = key_span.shape[1]
    queries_t = project_cols(w_query, normed).astype(jnp.bfloat16)
    keys_t = project_cols(w_key, normed).astype(jnp.bfloat16)
    values_t = project_cols(w_value, normed).astype(jnp.bfloat16)
    dout_t = lax.dot_general(
        w_out, grad_out, (((1,), (1,)), ((), ())), preferred_element_type=jnp.float32
    ).astype(jnp.bfloat16)
    paired_t = jnp.concatenate([keys_t, values_t], axis=0)
    paired_spans = jnp.transpose(paired_t.reshape(2 * col_count, owned, SPAN), (1, 0, 2))
    mirror_spans = lax.ppermute(paired_spans, "zh", swap)
    all_pairs = key_span.reshape(column_count, side_count, owned * per_reader)
    requests = lax.dynamic_index_in_dim(all_pairs, my_side, axis=1, keepdims=False)
    sides = my_column * side_count + jnp.arange(side_count, dtype=jnp.int32)
    hit = (requests // owned)[:, :, None] == sides[None, None, :]
    slot = jnp.sum(jnp.where(hit, (requests % owned)[:, :, None], 0), axis=1)
    exists = jnp.any(hit, axis=1)
    own_slot = lax.dynamic_index_in_dim(slot, my_side, axis=1, keepdims=False)
    mirror_slot = lax.dynamic_index_in_dim(slot, 1 - my_side, axis=1, keepdims=False)
    near = lax.all_to_all(paired_spans[own_slot], "tq", split_axis=0, concat_axis=0, tiled=True)
    far = lax.all_to_all(mirror_spans[mirror_slot], "tq", split_axis=0, concat_axis=0, tiled=True)
    own_ids = lax.dynamic_slice_in_dim(key_span, my_index * owned, owned, 0)
    owner_ids = (own_ids // owned).reshape(-1)
    owner_column = owner_ids // side_count
    from_near = owner_ids % side_count == my_side
    fetched = jnp.where(from_near[:, None, None], near[owner_column], far[owner_column])
    fetched = fetched.reshape(owned, per_reader, 2, head_count, HD, SPAN)
    query_rows = jnp.transpose(queries_t.reshape(head_count, HD, owned, SPAN), (2, 0, 1, 3))
    dout_rows = jnp.transpose(dout_t.reshape(head_count, HD, owned, SPAN), (2, 0, 1, 3))
    grad_query, grad_pair = attend_grad(
        query_rows, fetched[:, :, 0], fetched[:, :, 1], dout_rows
    )
    grad_query_t = jnp.transpose(grad_query, (1, 2, 0, 3)).reshape(col_count, row_count)
    query_term = project_back(grad_query_t, w_query)
    pair_grads = grad_pair.reshape(owned * per_reader, 2 * col_count, SPAN)
    pair_count = owned * per_reader
    pair_index = jnp.arange(pair_count, dtype=jnp.int32)
    unused = jnp.full((column_count,), pair_count, jnp.int32)
    near_pair = unused.at[jnp.where(from_near, owner_column, column_count)].set(pair_index, mode="drop")
    far_pair = unused.at[jnp.where(from_near, column_count, owner_column)].set(pair_index, mode="drop")
    picked = (
        exists[:, :, None] & (slot[:, :, None] == jnp.arange(owned, dtype=jnp.int32)[None, None, :])
    ).astype(jnp.bfloat16)
    far_back = lax.all_to_all(
        jnp.take(pair_grads, far_pair, axis=0, mode="clip"),
        "tq", split_axis=0, concat_axis=0, tiled=True,
    )
    other = jnp.einsum(
        "ck,crh->krh",
        lax.dynamic_index_in_dim(picked, 1 - my_side, axis=1, keepdims=False),
        far_back,
        preferred_element_type=jnp.float32,
    )
    other_back = lax.ppermute(other, "zh", swap)
    near_back = lax.all_to_all(
        jnp.take(pair_grads, near_pair, axis=0, mode="clip"),
        "tq", split_axis=0, concat_axis=0, tiled=True,
    )
    mine = jnp.einsum(
        "ck,crh->krh",
        lax.dynamic_index_in_dim(picked, my_side, axis=1, keepdims=False),
        near_back,
        preferred_element_type=jnp.float32,
    )
    summed = (mine + other_back).astype(jnp.bfloat16)
    summed_t = jnp.transpose(summed, (1, 0, 2)).reshape(2 * col_count, row_count)
    kv_term = project_back(summed_t[:col_count], w_key) + project_back(
        summed_t[col_count:], w_value
    )
    result = head_sum(query_term + kv_term)
    return result


def solution(mesh):
    tm_size = mesh.shape["tm"]
    tensor_size = mesh.shape["tensor"]
    split = Mesh(mesh.devices.reshape(tm_size // 2, 2, tensor_size), ("tq", "zh", "tensor"))
    rows = P(("tq", "zh"), None)
    return jax.shard_map(
        local,
        mesh=split,
        in_specs=(
            rows,
            rows,
            P(None, "tensor"),
            P(None, "tensor"),
            P(None, "tensor"),
            P("tensor", None),
            P(),
        ),
        out_specs=rows,
        check_vma=False,
    )
```

```python
import jax
import jax.numpy as jnp
from jax import lax
from jax.sharding import Mesh, PartitionSpec as P

HD = 64
SPAN = 128


def attend_grad(query_t, key_t, value_t, dout_t):
    scaling = HD ** (-0.5)
    scores = (
        jnp.einsum("chdq,cjhdk->chqjk", query_t, key_t, preferred_element_type=jnp.float32)
        * scaling
    )
    probs = jax.nn.softmax(scores, axis=(-2, -1))
    probs_b = probs.astype(jnp.bfloat16)
    attn = jnp.einsum("chqjk,cjhdk->chdq", probs_b, value_t, preferred_element_type=jnp.float32)
    delta = jnp.sum(dout_t.astype(jnp.float32) * attn, axis=2)
    dprobs = jnp.einsum("chdq,cjhdk->chqjk", dout_t, value_t, preferred_element_type=jnp.float32)
    dscores_b = (probs * (dprobs - delta[:, :, :, None, None])).astype(jnp.bfloat16)
    grad_query = (
        jnp.einsum("chqjk,cjhdk->chdq", dscores_b, key_t, preferred_element_type=jnp.float32)
        * scaling
    ).astype(jnp.bfloat16)
    grad_pair = jnp.einsum(
        "gchqjk,gchdq->cjghdk",
        jnp.stack([dscores_b, probs_b]),
        jnp.stack([query_t * scaling, dout_t]),
        preferred_element_type=jnp.float32,
    ).astype(jnp.bfloat16)
    return (grad_query, grad_pair)


def project_back(grads_t, weight):
    return lax.dot_general(
        grads_t, weight, (((0,), (1,)), ((), ())), preferred_element_type=jnp.float32
    )


def project_cols(weight, inputs):
    return lax.dot_general(
        weight, inputs, (((0,), (1,)), ((), ())), preferred_element_type=jnp.float32
    )


def head_sum(partial):
    index = lax.axis_index("tensor")
    count = lax.axis_size("tensor")
    cur = partial
    step = 1
    while step < count:
        upper = (index & step) != 0
        half = cur.shape[0] // 2
        low, high = cur[:half], cur[half:]
        keep = jnp.where(upper, high, low)
        send = jnp.where(upper, low, high)
        got = lax.ppermute(send.astype(jnp.bfloat16), "tensor", [(i, i ^ step) for i in range(count)])
        cur = keep + got.astype(jnp.float32)
        step *= 2
    cur = cur.astype(jnp.bfloat16)
    while step > 1:
        step //= 2
        upper = (index & step) != 0
        got = lax.ppermute(cur, "tensor", [(i, i ^ step) for i in range(count)])
        cur = jnp.where(upper, jnp.concatenate([got, cur]), jnp.concatenate([cur, got]))
    return cur.astype(jnp.float32)


def local(normed, grad_out, w_query, w_key, w_value, w_out, key_span):
    column_count = lax.axis_size("tq")
    side_count = lax.axis_size("zh")
    my_column = lax.axis_index("tq")
    my_side = lax.axis_index("zh")
    device_count = column_count * side_count
    my_index = my_column * side_count + my_side
    swap = [(0, 1), (1, 0)]
    row_count = normed.shape[0]
    col_count = w_query.shape[1]
    head_count = col_count // HD
    owned = row_count // SPAN
    per_reader = key_span.shape[1]
    queries_t = project_cols(w_query, normed).astype(jnp.bfloat16)
    keys_t = project_cols(w_key, normed).astype(jnp.bfloat16)
    values_t = project_cols(w_value, normed).astype(jnp.bfloat16)
    dout_t = lax.dot_general(
        w_out, grad_out, (((1,), (1,)), ((), ())), preferred_element_type=jnp.float32
    ).astype(jnp.bfloat16)
    paired_t = jnp.concatenate([keys_t, values_t], axis=0)
    paired_spans = jnp.transpose(paired_t.reshape(2 * col_count, owned, SPAN), (1, 0, 2))
    mirror_spans = lax.ppermute(paired_spans, "zh", swap)
    all_pairs = key_span.reshape(column_count, side_count, owned * per_reader)
    requests = lax.dynamic_index_in_dim(all_pairs, my_side, axis=1, keepdims=False)
    sides = my_column * side_count + jnp.arange(side_count, dtype=jnp.int32)
    hit = (requests // owned)[:, :, None] == sides[None, None, :]
    slot = jnp.sum(jnp.where(hit, (requests % owned)[:, :, None], 0), axis=1)
    exists = jnp.any(hit, axis=1)
    own_slot = lax.dynamic_index_in_dim(slot, my_side, axis=1, keepdims=False)
    mirror_slot = lax.dynamic_index_in_dim(slot, 1 - my_side, axis=1, keepdims=False)
    near = lax.all_to_all(paired_spans[own_slot], "tq", split_axis=0, concat_axis=0, tiled=True)
    far = lax.all_to_all(mirror_spans[mirror_slot], "tq", split_axis=0, concat_axis=0, tiled=True)
    own_ids = lax.dynamic_slice_in_dim(key_span, my_index * owned, owned, 0)
    owner_ids = (own_ids // owned).reshape(-1)
    owner_column = owner_ids // side_count
    from_near = owner_ids % side_count == my_side
    near_picked = lax.optimization_barrier(near[owner_column])
    fetched = jnp.where(from_near[:, None, None], near_picked, far[owner_column])
    fetched = fetched.reshape(owned, per_reader, 2, head_count, HD, SPAN)
    query_rows = jnp.transpose(queries_t.reshape(head_count, HD, owned, SPAN), (2, 0, 1, 3))
    dout_rows = jnp.transpose(dout_t.reshape(head_count, HD, owned, SPAN), (2, 0, 1, 3))
    grad_query, grad_pair = attend_grad(
        query_rows, fetched[:, :, 0], fetched[:, :, 1], dout_rows
    )
    grad_query_t = jnp.transpose(grad_query, (1, 2, 0, 3)).reshape(col_count, row_count)
    query_term = project_back(grad_query_t, w_query)
    pair_grads = grad_pair.reshape(owned * per_reader, 2 * col_count, SPAN)
    pair_count = owned * per_reader
    pair_index = jnp.arange(pair_count, dtype=jnp.int32)
    unused = jnp.full((column_count,), pair_count, jnp.int32)
    near_pair = unused.at[jnp.where(from_near, owner_column, column_count)].set(pair_index, mode="drop")
    far_pair = unused.at[jnp.where(from_near, column_count, owner_column)].set(pair_index, mode="drop")
    picked = (
        exists[:, :, None] & (slot[:, :, None] == jnp.arange(owned, dtype=jnp.int32)[None, None, :])
    ).astype(jnp.bfloat16)
    far_back = lax.all_to_all(
        jnp.take(pair_grads, far_pair, axis=0, mode="clip"),
        "tq", split_axis=0, concat_axis=0, tiled=True,
    )
    other = jnp.einsum(
        "ck,crh->krh",
        lax.dynamic_index_in_dim(picked, 1 - my_side, axis=1, keepdims=False),
        far_back,
        preferred_element_type=jnp.float32,
    )
    other_back = lax.ppermute(other, "zh", swap)
    near_back = lax.all_to_all(
        jnp.take(pair_grads, near_pair, axis=0, mode="clip"),
        "tq", split_axis=0, concat_axis=0, tiled=True,
    )
    mine = jnp.einsum(
        "ck,crh->krh",
        lax.dynamic_index_in_dim(picked, my_side, axis=1, keepdims=False),
        near_back,
        preferred_element_type=jnp.float32,
    )
    summed = (mine + other_back).astype(jnp.bfloat16)
    summed_t = jnp.transpose(summed, (1, 0, 2)).reshape(2 * col_count, row_count)
    kv_term = project_back(summed_t[:col_count], w_key) + project_back(
        summed_t[col_count:], w_value
    )
    result = head_sum(query_term + kv_term)
    return result


def solution(mesh):
    tm_size = mesh.shape["tm"]
    tensor_size = mesh.shape["tensor"]
    split = Mesh(mesh.devices.reshape(tm_size // 2, 2, tensor_size), ("tq", "zh", "tensor"))
    rows = P(("tq", "zh"), None)
    return jax.shard_map(
        local,
        mesh=split,
        in_specs=(
            rows,
            rows,
            P(None, "tensor"),
            P(None, "tensor"),
            P(None, "tensor"),
            P("tensor", None),
            P(),
        ),
        out_specs=rows,
        check_vma=False,
    )
```

```python
import jax
import jax.numpy as jnp
from jax import lax
from jax.sharding import Mesh, PartitionSpec as P

HD = 64
SPAN = 128


def attend_grad(query_t, key_t, value_t, dout_t):
    scaling = HD ** (-0.5)
    scores = (
        jnp.einsum("chdq,cjhdk->chqjk", query_t, key_t, preferred_element_type=jnp.float32)
        * scaling
    )
    probs = jax.nn.softmax(scores, axis=(-2, -1))
    probs_b = probs.astype(jnp.bfloat16)
    attn = jnp.einsum("chqjk,cjhdk->chdq", probs_b, value_t, preferred_element_type=jnp.float32)
    delta = jnp.sum(dout_t.astype(jnp.float32) * attn, axis=2)
    dprobs = jnp.einsum("chdq,cjhdk->chqjk", dout_t, value_t, preferred_element_type=jnp.float32)
    dscores_b = (probs * (dprobs - delta[:, :, :, None, None])).astype(jnp.bfloat16)
    grad_query = (
        jnp.einsum("chqjk,cjhdk->chdq", dscores_b, key_t, preferred_element_type=jnp.float32)
        * scaling
    ).astype(jnp.bfloat16)
    grad_pair = jnp.einsum(
        "gchqjk,gchdq->cjghdk",
        jnp.stack([dscores_b, probs_b]),
        jnp.stack([query_t * scaling, dout_t]),
        preferred_element_type=jnp.float32,
    ).astype(jnp.bfloat16)
    return (grad_query, grad_pair)


def project_back(grads_t, weight):
    return lax.dot_general(
        grads_t, weight, (((0,), (1,)), ((), ())), preferred_element_type=jnp.float32
    )


def project_cols(weight, inputs):
    return lax.dot_general(
        weight, inputs, (((0,), (1,)), ((), ())), preferred_element_type=jnp.float32
    )


def head_sum(partial):
    index = lax.axis_index("tensor")
    count = lax.axis_size("tensor")
    cur = partial
    step = 1
    while step < count:
        upper = (index & step) != 0
        half = cur.shape[0] // 2
        keep = lax.dynamic_slice_in_dim(cur, upper.astype(jnp.int32) * half, half, 0)
        send = lax.dynamic_slice_in_dim(cur, (1 - upper.astype(jnp.int32)) * half, half, 0)
        got = lax.ppermute(send.astype(jnp.bfloat16), "tensor", [(i, i ^ step) for i in range(count)])
        cur = keep + got.astype(jnp.float32)
        step *= 2
    cur = cur.astype(jnp.bfloat16)
    while step > 1:
        step //= 2
        upper = (index & step) != 0
        got = lax.ppermute(cur, "tensor", [(i, i ^ step) for i in range(count)])
        cur = jnp.where(upper, jnp.concatenate([got, cur]), jnp.concatenate([cur, got]))
    return cur.astype(jnp.float32)


def local(normed, grad_out, w_query, w_key, w_value, w_out, key_span):
    column_count = lax.axis_size("tq")
    side_count = lax.axis_size("zh")
    my_column = lax.axis_index("tq")
    my_side = lax.axis_index("zh")
    device_count = column_count * side_count
    my_index = my_column * side_count + my_side
    swap = [(0, 1), (1, 0)]
    row_count = normed.shape[0]
    col_count = w_query.shape[1]
    head_count = col_count // HD
    owned = row_count // SPAN
    per_reader = key_span.shape[1]
    queries_t = project_cols(w_query, normed).astype(jnp.bfloat16)
    keys_t = project_cols(w_key, normed).astype(jnp.bfloat16)
    values_t = project_cols(w_value, normed).astype(jnp.bfloat16)
    dout_t = lax.dot_general(
        w_out, grad_out, (((1,), (1,)), ((), ())), preferred_element_type=jnp.float32
    ).astype(jnp.bfloat16)
    paired_t = jnp.concatenate([keys_t, values_t], axis=0)
    paired_spans = jnp.transpose(paired_t.reshape(2 * col_count, owned, SPAN), (1, 0, 2))
    mirror_spans = lax.ppermute(paired_spans, "zh", swap)
    all_pairs = key_span.reshape(column_count, side_count, owned * per_reader)
    requests = lax.dynamic_index_in_dim(all_pairs, my_side, axis=1, keepdims=False)
    sides = my_column * side_count + jnp.arange(side_count, dtype=jnp.int32)
    hit = (requests // owned)[:, :, None] == sides[None, None, :]
    slot = jnp.sum(jnp.where(hit, (requests % owned)[:, :, None], 0), axis=1)
    exists = jnp.any(hit, axis=1)
    own_slot = lax.dynamic_index_in_dim(slot, my_side, axis=1, keepdims=False)
    mirror_slot = lax.dynamic_index_in_dim(slot, 1 - my_side, axis=1, keepdims=False)
    near = lax.all_to_all(paired_spans[own_slot], "tq", split_axis=0, concat_axis=0, tiled=True)
    far = lax.all_to_all(mirror_spans[mirror_slot], "tq", split_axis=0, concat_axis=0, tiled=True)
    own_ids = lax.dynamic_slice_in_dim(key_span, my_index * owned, owned, 0)
    owner_ids = (own_ids // owned).reshape(-1)
    owner_column = owner_ids // side_count
    from_near = owner_ids % side_count == my_side
    near_picked = lax.optimization_barrier(near[owner_column])
    fetched = jnp.where(from_near[:, None, None], near_picked, far[owner_column])
    fetched = fetched.reshape(owned, per_reader, 2, head_count, HD, SPAN)
    query_rows = jnp.transpose(queries_t.reshape(head_count, HD, owned, SPAN), (2, 0, 1, 3))
    dout_rows = jnp.transpose(dout_t.reshape(head_count, HD, owned, SPAN), (2, 0, 1, 3))
    grad_query, grad_pair = attend_grad(
        query_rows, fetched[:, :, 0], fetched[:, :, 1], dout_rows
    )
    grad_query_t = jnp.transpose(grad_query, (1, 2, 0, 3)).reshape(col_count, row_count)
    query_term = project_back(grad_query_t, w_query)
    pair_grads = grad_pair.reshape(owned * per_reader, 2 * col_count, SPAN)
    pair_count = owned * per_reader
    pair_index = jnp.arange(pair_count, dtype=jnp.int32)
    unused = jnp.full((column_count,), pair_count, jnp.int32)
    near_pair = unused.at[jnp.where(from_near, owner_column, column_count)].set(pair_index, mode="drop")
    far_pair = unused.at[jnp.where(from_near, column_count, owner_column)].set(pair_index, mode="drop")
    picked = (
        exists[:, :, None] & (slot[:, :, None] == jnp.arange(owned, dtype=jnp.int32)[None, None, :])
    ).astype(jnp.bfloat16)
    far_back = lax.all_to_all(
        jnp.take(pair_grads, far_pair, axis=0, mode="clip"),
        "tq", split_axis=0, concat_axis=0, tiled=True,
    )
    other = jnp.einsum(
        "ck,crh->krh",
        lax.dynamic_index_in_dim(picked, 1 - my_side, axis=1, keepdims=False),
        far_back,
        preferred_element_type=jnp.float32,
    )
    other_back = lax.ppermute(other, "zh", swap)
    near_back = lax.all_to_all(
        jnp.take(pair_grads, near_pair, axis=0, mode="clip"),
        "tq", split_axis=0, concat_axis=0, tiled=True,
    )
    mine = jnp.einsum(
        "ck,crh->krh",
        lax.dynamic_index_in_dim(picked, my_side, axis=1, keepdims=False),
        near_back,
        preferred_element_type=jnp.float32,
    )
    summed = (mine + other_back).astype(jnp.bfloat16)
    summed_t = jnp.transpose(summed, (1, 0, 2)).reshape(2 * col_count, row_count)
    kv_term = project_back(summed_t[:col_count], w_key) + project_back(
        summed_t[col_count:], w_value
    )
    result = head_sum(query_term + kv_term)
    return result


def solution(mesh):
    tm_size = mesh.shape["tm"]
    tensor_size = mesh.shape["tensor"]
    split = Mesh(mesh.devices.reshape(tm_size // 2, 2, tensor_size), ("tq", "zh", "tensor"))
    rows = P(("tq", "zh"), None)
    return jax.shard_map(
        local,
        mesh=split,
        in_specs=(
            rows,
            rows,
            P(None, "tensor"),
            P(None, "tensor"),
            P(None, "tensor"),
            P("tensor", None),
            P(),
        ),
        out_specs=rows,
        check_vma=False,
    )
```
